512 devices in a mesh: req: 128 (over z, y, core), tp: 4 (over x).
Axes of the slice: x: 4, y: 4, z: 16, core: 2. Of those that a mesh axis runs over, the one named last changes fastest.
Arguments:
- query: bfloat16 [512, 2304], P('req', 'tp'), may hold values from -6 to 6
- new_key: bfloat16 [512, 2304], P('req', 'tp'), may hold values from -6 to 6
- new_value: bfloat16 [512, 2304], P('req', 'tp'), may hold values from -6 to 6
- key_cache: bfloat16 [512, 128, 2304], P('req', None, 'tp'), may hold values from -6 to 6
- value_cache: bfloat16 [512, 128, 2304], P('req', None, 'tp'), may hold values from -6 to 6
- lengths: int32 [512], P('req'), may hold values from 1 to 128, 32768 in all
- resid: bfloat16 [512, 2304], P('req'), may hold values from -6 to 6
- out_weight: bfloat16 [2304, 2304], P('tp'), may hold values from -0.125 to 0.125
- norm_gain: float32 [2304], P('tp'), may hold values from 0.25 to 1.75
- expert_ids: int32 [512, 2], replicated, may hold values from 0 to 7, all different within a row; in each aligned block of 4 rows (0 to 3, 4 to 7, ...) at most 2 rows name the same one
- route_weight: float32 [512, 2], replicated, may hold values from 0.2 to 1
- gate_weight: bfloat16 [2304, 46080], P('tp', 'req'), may hold values from -0.125 to 0.125
- up_weight: bfloat16 [2304, 46080], P('tp', 'req'), may hold values from -0.125 to 0.125
- down_weight: bfloat16 [46080, 2304], P('req', 'tp'), may hold values from -0.078125 to 0.078125
Outputs:
- layer_out: bfloat16 [512, 2304], P('req', 'tp')
The draws below stay inside these ranges and needn't reach their ends.
Inputs may be any that keep to these rules, and one draw needn't show every extreme that they name: `lengths`: each request has 1 to 128 valid cached positions, and some request has exactly 128. `expert_ids`: the two experts of a token differ, every expert is chosen by some token, and in each aligned block of 4 rows (the rows of one device) no expert is chosen by more than 2 rows; in some block one expert is chosen by exactly 2 rows.
All inputs are finite; a program needn't handle non-finite values. No bound on the sum of `lengths` on one device may be relied on, other than what follows from the above.
Results may differ from the reference program's by a relative error of at most 0.007.
Values may be sent and summed in bfloat16 or wider, within the bound.
No kernel may reach another device: no remote copies, remote signals or barrier semaphores. Data moves between devices by JAX's collectives and lax.ppermute only.
A program may use at most 64 MiB of HBM per device.

```python
import math
import jax
import jax.numpy as jnp
import numpy as np
from jax import lax

D = 2304
HEADS = 36
HD = 64
EXPERTS = 8
FF = 5760
TOPK = 2
REQ_DEV = 4
CACHE = 128
CAP = 2
REQ = 512


def draw_query(key, part):
    values = jnp.clip(jax.random.normal(jax.random.fold_in(key, 1), (REQ, D), jnp.float32), -6.0, 6.0)
    return values.astype(jnp.bfloat16)


def draw_new_key(key, part):
    values = jnp.clip(jax.random.normal(jax.random.fold_in(key, 2), (REQ, D), jnp.float32), -6.0, 6.0)
    return values.astype(jnp.bfloat16)


def draw_key_cache(key, part):
    values = jnp.clip(jax.random.normal(jax.random.fold_in(key, 3), (REQ, CACHE, D), jnp.float32), -6.0, 6.0)
    return values.astype(jnp.bfloat16)


def level_of(own_key, extent, cuts, low, largest):
    gain, own = 1.0, jax.random.fold_in(own_key, 6)
    for axis_at, blocks in cuts:
        steps = jnp.exp(jax.random.uniform(jax.random.fold_in(own, axis_at), (blocks,), jnp.float32, low / len(cuts), largest / len(cuts)))
        gain = gain * jnp.repeat(steps, extent[axis_at] // blocks).reshape([-1 if axis == axis_at else 1 for axis in range(len(extent))])
    return gain


def profile(amount, total, reach, skew):
    weights = [(1 << 20) // math.isqrt(grade ** skew) + 1 for grade in range(2, amount + 1)]
    rest, given = total - reach - (amount - 1), [1] * (amount - 1)
    while rest > 0:
        free = [i for i in range(amount - 1) if given[i] < reach]
        mass, budget = sum([weights[i] for i in free]), rest
        for i in free:
            addition = min(reach - given[i], max(1, budget * weights[i] // mass), rest)
            given[i] = given[i] + addition
            rest = rest - addition
    return np.array([reach] + given)


def uneven(rng, number_of, total, most, skew):
    if number_of == 2:
        one = jax.random.randint(rng, (), max(1, total - most), min(most, total - 1) + 1)
        return jnp.stack([one, total - one])
    sizes = jnp.asarray(profile(number_of, total, most, skew), jnp.int32)
    pairs = (number_of - 1) // 2
    donor, taker = sizes[1:1 + 2 * pairs:2], sizes[2:2 + 2 * pairs:2]
    slack = jnp.minimum(donor - 1, most - taker)
    shifted = jax.random.randint(jax.random.fold_in(rng, 1), (pairs,), 0, 1 << 20) % (slack + 1)
    sizes = sizes.at[1:1 + 2 * pairs:2].set(donor - shifted).at[2:2 + 2 * pairs:2].set(taker + shifted)
    return sizes[jax.random.permutation(jax.random.fold_in(rng, 2), number_of)]


def shared_out(key, own, number, rows, count, top, most, skew):
    ranking = jax.random.permutation(key, count)
    packed, common = load_shares(count, rows * top, most, skew, True), load_shares(count, rows * top, most, skew, False)
    places = jnp.arange(count)

    def named(sizes, offset_by):
        used = int((sizes > 0).sum())
        fixed = max(1, used // 4)
        passed = fixed + (places - fixed + offset_by * (used - fixed)) % max(1, count - fixed)
        return jnp.zeros((count,), jnp.int32).at[ranking[jnp.where(places < fixed, places, passed)]].set(jnp.asarray(sizes, jnp.int32))

    sizes = jnp.where(number % 4 == 0, named(packed, number // 4), named(common, number - number // 4 - 1))
    mixed = jax.random.permutation(jax.random.fold_in(own, 3), count)
    source_of, receiver = mixed[0:count // 2 * 2:2], mixed[1:count // 2 * 2:2]
    margin = jnp.minimum(sizes[source_of] - 1, most - sizes[receiver]) // 2
    margin = jnp.where((source_of == ranking[0]) | (receiver == ranking[0]) | (sizes[receiver] == 0), 0, jnp.maximum(margin, 0))
    passed = jax.random.randint(jax.random.fold_in(own, 4), (count // 2,), 0, 1 << 20) % (margin + 1)
    sizes = sizes.at[source_of].add(-passed).at[receiver].add(passed)
    labels = jnp.searchsorted(jnp.cumsum(sizes), jnp.arange(rows * top), side="right").astype(jnp.int32)
    table = labels.reshape(top, rows).T
    table = table[jax.random.permutation(jax.random.fold_in(own, 1), rows)]
    offset_by = jax.random.randint(jax.random.fold_in(own, 2), (rows, 1), 0, top)
    return jnp.take_along_axis(table, (jnp.arange(top)[None, :] + offset_by) % top, axis=1)


def load_shares(amount, total, reach, lean, full):
    loads = [(1 << 20) // math.isqrt(rank ** lean) + 1 for rank in range(1, amount + 1)]
    largest = reach if full else min(reach, max(-(-total // amount), total * loads[0] // sum(loads)))
    least = 1 if total - largest >= amount - 1 else 0
    counts, spare = [largest] + [least] * (amount - 1), total - largest - least * (amount - 1)
    while spare > 0:
        free = [i for i in range(1, amount) if counts[i] < largest] or [i for i in range(1, amount) if counts[i] < reach]
        whole, budget = sum([loads[i] for i in free]), spare
        for i in free:
            more = min(reach - counts[i], max(1, budget * loads[i] // whole), spare)
            counts[i] = counts[i] + more
            spare = spare - more
    return np.array(counts)


def scatter_about(own_key, shape, spread, reach, shards=(), held_as=jnp.bfloat16):
    array = spread * jax.random.normal(own_key, shape, jnp.float32)
    if shards:
        array = array * level_of(own_key, shape, shards, -0.22, 0.18)
    return jnp.clip(array, -reach, reach).astype(held_as)


def setup_inputs(seed: int = 0) -> dict:
    arg_keys = jax.random.split(jax.random.key(seed), 15)
    query = draw_query(jax.random.fold_in(arg_keys[14], 71), 0)
    new_key = draw_new_key(jax.random.fold_in(arg_keys[14], 71), 0)
    new_value = scatter_about(arg_keys[2], (REQ, D), 1.0, 6.0, ((0, 128), (1, 4)))
    key_cache = draw_key_cache(jax.random.fold_in(arg_keys[14], 71), 0)
    value_cache = scatter_about(arg_keys[4], (REQ, CACHE, D), 1.0, 6.0, ((0, 128), (2, 4)))
    lengths = uneven(arg_keys[5], REQ, REQ * CACHE // 2, CACHE, 2).astype(jnp.int32)
    resid = scatter_about(arg_keys[6], (REQ, D), 1.0, 6.0, ((0, 128),))
    out_weight = scatter_about(arg_keys[7], (D, D), D ** -0.5, 0.125, ((0, 4),))
    norm_gain = jnp.clip(1.0 + 0.15 * jax.random.normal(arg_keys[8], (D,), jnp.float32), 0.25, 1.75)
    expert_ids_keys = jax.random.split(jax.random.fold_in(arg_keys[9], 1), REQ // REQ_DEV)
    expert_ids_turns = jax.random.permutation(jax.random.fold_in(arg_keys[9], 3), REQ // REQ_DEV)
    expert_ids = jax.vmap(lambda own, number: shared_out(jax.random.fold_in(arg_keys[9], 2), own, number, REQ_DEV, EXPERTS, TOPK, CAP, 2))(expert_ids_keys, expert_ids_turns).reshape((REQ, TOPK))
    route_weight = jnp.clip(jax.random.uniform(arg_keys[10], (REQ, TOPK), jnp.float32, 0.2, 1.0), 0.2, 1.0)
    gate_weight = scatter_about(arg_keys[11], (D, EXPERTS * FF), D ** -0.5, 0.125, ((0, 4), (1, 128)))
    up_weight = scatter_about(arg_keys[12], (D, EXPERTS * FF), D ** -0.5, 0.125, ((0, 4), (1, 128)))
    down_weight = scatter_about(arg_keys[13], (EXPERTS * FF, D), FF ** -0.5, 0.078125, ((0, 128), (1, 4)))
    return {"query": query, "new_key": new_key, "new_value": new_value, "key_cache": key_cache, "value_cache": value_cache, "lengths": lengths, "resid": resid, "out_weight": out_weight, "norm_gain": norm_gain, "expert_ids": expert_ids, "route_weight": route_weight, "gate_weight": gate_weight, "up_weight": up_weight, "down_weight": down_weight}


def attention(query, new_key, new_value, key_cache, value_cache, lengths):
    score_scale = HD ** (-0.5)
    queries = query.astype(jnp.float32).reshape(REQ, HEADS, HD)
    cached_keys = key_cache.astype(jnp.float32).reshape(REQ, CACHE, HEADS, HD)
    cached_values = value_cache.astype(jnp.float32).reshape(REQ, CACHE, HEADS, HD)
    scores = jnp.einsum('rhd,rjhd->rhj', queries, cached_keys) * score_scale
    own_score = lax.optimization_barrier(jnp.sum(queries * new_key.astype(jnp.float32).reshape(REQ, HEADS, HD), axis=-1)) * score_scale
    positions = jnp.arange(CACHE, dtype=jnp.int32)
    is_valid = positions[None, None, :] < lengths.astype(jnp.int32)[:, None, None]
    scores = jnp.where(is_valid, scores, -jnp.inf)
    highest = jnp.maximum(lax.optimization_barrier(jnp.max(scores, axis=-1)), own_score)
    cached_exp = jnp.exp(scores - highest[..., None])
    own_exp = jnp.exp(own_score - highest)
    denominator = lax.optimization_barrier(jnp.sum(cached_exp, axis=-1)) + own_exp
    cached_prob = (cached_exp / denominator[..., None]).astype(jnp.bfloat16)
    own_prob = (own_exp / denominator).astype(jnp.bfloat16)
    mixed_values = jnp.einsum('rhj,rjhd->rhd', cached_prob.astype(jnp.float32), cached_values)
    mixed_values = mixed_values + own_prob.astype(jnp.float32)[..., None] * new_value.astype(jnp.float32).reshape(REQ, HEADS, HD)
    return mixed_values.reshape(REQ, D).astype(jnp.bfloat16)

def reference(query, new_key, new_value, key_cache, value_cache, lengths, resid, out_weight, norm_gain, expert_ids, route_weight, gate_weight, up_weight, down_weight):
    attn_out = attention(query, new_key, new_value, key_cache, value_cache, lengths)
    hidden_state = resid.astype(jnp.float32) + jnp.dot(attn_out, out_weight, preferred_element_type=jnp.float32)
    mean_square = lax.optimization_barrier(jnp.mean(hidden_state * hidden_state, axis=1, keepdims=True))
    normed = (hidden_state * lax.rsqrt(mean_square + 1e-05) * norm_gain[None, :]).astype(jnp.bfloat16)
    moe_sum = jnp.zeros((REQ, D), jnp.float32)
    for expert in range(EXPERTS):
        gate_part = jnp.dot(normed, gate_weight[:, expert * FF:(expert + 1) * FF], preferred_element_type=jnp.float32)
        up_part = jnp.dot(normed, up_weight[:, expert * FF:(expert + 1) * FF], preferred_element_type=jnp.float32)
        activ = (jax.nn.silu(gate_part) * up_part).astype(jnp.bfloat16)
        expert_out = jnp.dot(activ, down_weight[expert * FF:(expert + 1) * FF, :], preferred_element_type=jnp.float32)
        route_share = lax.optimization_barrier(jnp.sum(jnp.where(expert_ids == expert, route_weight, 0.0), axis=1))
        moe_sum = moe_sum + route_share[:, None] * expert_out
    return (hidden_state + moe_sum).astype(jnp.bfloat16)
```

```python
import jax
import jax.numpy as jnp
from jax import lax
from jax.sharding import PartitionSpec as P

HD = 64
EXPERTS = 8


def local_attention(query, new_key, new_value, key_cache, value_cache, lengths):
    row_count = query.shape[0]
    local_width = query.shape[1]
    head_count = local_width // HD
    cache_len = key_cache.shape[1]
    score_scale = HD ** (-0.5)
    queries = query.reshape(row_count, head_count, HD)
    cached_keys = key_cache.reshape(row_count, cache_len, head_count, HD)
    cached_values = value_cache.reshape(row_count, cache_len, head_count, HD)
    scores = (
        jnp.einsum("rhd,rjhd->rhj", queries, cached_keys, preferred_element_type=jnp.float32)
        * score_scale
    )
    own_score = (
        jnp.sum(
            queries.astype(jnp.float32)
            * new_key.reshape(row_count, head_count, HD).astype(jnp.float32),
            axis=-1,
        )
        * score_scale
    )
    positions = jnp.arange(cache_len, dtype=jnp.int32)
    is_valid = positions[None, None, :] < lengths[:, None, None]
    scores = jnp.where(is_valid, scores, -jnp.inf)
    highest = jnp.maximum(jnp.max(scores, axis=-1), own_score)
    cached_exp = jnp.exp(scores - highest[..., None])
    own_exp = jnp.exp(own_score - highest)
    denominator = jnp.sum(cached_exp, axis=-1) + own_exp
    cached_prob = (cached_exp / denominator[..., None]).astype(jnp.bfloat16)
    own_prob = (own_exp / denominator).astype(jnp.bfloat16)
    mixed_values = jnp.einsum(
        "rhj,rjhd->rhd", cached_prob, cached_values, preferred_element_type=jnp.float32
    )
    mixed_values = mixed_values + own_prob.astype(jnp.float32)[..., None] * new_value.reshape(
        row_count, head_count, HD
    ).astype(jnp.float32)
    return mixed_values.reshape(row_count, local_width).astype(jnp.bfloat16)


def slot_tables(block_ids, block_weights, capacity):
    blocks, rows, picks = block_ids.shape
    expert_hit = block_ids[..., None] == jnp.arange(EXPERTS, dtype=jnp.int32)
    flat_hits = expert_hit.reshape(blocks, rows * picks, EXPERTS).astype(jnp.int32)
    earlier = jnp.cumsum(flat_hits, axis=1) - flat_hits
    slot_index = jnp.sum(earlier * flat_hits, axis=-1).reshape(blocks, rows, picks)
    slot_hit = slot_index[..., None] == jnp.arange(capacity, dtype=jnp.int32)
    pair_hit = expert_hit[..., :, None] & slot_hit[..., None, :]
    selector = jnp.any(pair_hit, axis=2).astype(jnp.bfloat16)
    combiner = jnp.sum(jnp.where(pair_hit, block_weights[..., None, None], 0.0), axis=2)
    return (selector, combiner)


def shards(
    query,
    new_key,
    new_value,
    key_cache,
    value_cache,
    lengths,
    resid,
    out_weight,
    norm_gain,
    expert_ids,
    route_weight,
    gate_weight,
    up_weight,
    down_weight,
):
    row_count = query.shape[0]
    attn_out = local_attention(query, new_key, new_value, key_cache, value_cache, lengths)
    model_width = out_weight.shape[1]
    share = model_width // lax.axis_size("tp")
    col_start = lax.axis_index("tp") * share
    resid_float = resid.astype(jnp.float32)
    proj_part = jnp.dot(attn_out, out_weight, preferred_element_type=jnp.float32)
    proj_all = lax.all_gather(proj_part, "tp", axis=0, tiled=False)
    hidden_full = resid_float + jnp.sum(proj_all, axis=0)
    mean_square = jnp.mean(hidden_full * hidden_full, axis=1)
    inv_rms = lax.rsqrt(mean_square + 1e-05)
    hidden_state = lax.dynamic_slice_in_dim(hidden_full, col_start, share, 1)
    normed = (hidden_state * inv_rms[:, None] * norm_gain[None, :]).astype(jnp.bfloat16)
    req_count = lax.axis_size("req")
    group_size = req_count // EXPERTS
    capacity = max(2, row_count // 2)
    first_row = lax.axis_index("req") * row_count
    my_ids = lax.dynamic_slice_in_dim(expert_ids, first_row, row_count, 0)
    my_weights = lax.dynamic_slice_in_dim(route_weight, first_row, row_count, 0)
    selector, combiner = slot_tables(my_ids[None], my_weights[None], capacity)
    expert_rows = jnp.einsum(
        "tec,tf->ecf", selector[0], normed, preferred_element_type=jnp.float32
    ).astype(jnp.bfloat16)
    outgoing = jnp.repeat(expert_rows, group_size, axis=0)
    arrived = lax.all_to_all(outgoing, "req", split_axis=0, concat_axis=0, tiled=True)
    token_rows = arrived.reshape(req_count * capacity, share)
    gate_part = jnp.dot(token_rows, gate_weight, preferred_element_type=jnp.float32)
    up_part = jnp.dot(token_rows, up_weight, preferred_element_type=jnp.float32)
    gate_part, up_part = lax.psum((gate_part, up_part), "tp")
    activ = (jax.nn.silu(gate_part) * up_part).astype(jnp.bfloat16)
    partial_out = (
        jnp.dot(activ, down_weight, preferred_element_type=jnp.float32)
        .astype(jnp.bfloat16)
        .reshape(req_count, capacity, share)
    )
    returned = lax.all_to_all(partial_out, "req", split_axis=0, concat_axis=0, tiled=True)
    grouped = jnp.sum(
        returned.reshape(EXPERTS, group_size, capacity, share).astype(jnp.float32), axis=1
    )
    moe_sum = jnp.einsum("tec,ecf->tf", combiner[0], grouped, precision=lax.Precision.HIGHEST)
    return (hidden_state + moe_sum).astype(jnp.bfloat16)


def solution(mesh):
    placed = (
        P("req", "tp"),
        P("req", "tp"),
        P("req", "tp"),
        P("req", None, "tp"),
        P("req", None, "tp"),
        P("req"),
        P("req", None),
        P("tp", None),
        P("tp"),
        P(),
        P(),
        P("tp", "req"),
        P("tp", "req"),
        P("req", "tp"),
    )
    return jax.shard_map(
        shards, mesh=mesh, in_specs=placed, out_specs=P("req", "tp"), check_vma=False
    )
```

```python
import jax
import jax.numpy as jnp
from jax import lax
from jax.sharding import PartitionSpec as P

HD = 64
EXPERTS = 8


def local_attention(query, new_key, new_value, key_cache, value_cache, lengths):
    row_count = query.shape[0]
    local_width = query.shape[1]
    head_count = local_width // HD
    cache_len = key_cache.shape[1]
    score_scale = HD ** (-0.5)
    queries = query.reshape(row_count, head_count, HD)
    cached_keys = key_cache.reshape(row_count, cache_len, head_count, HD)
    cached_values = value_cache.reshape(row_count, cache_len, head_count, HD)
    scores = (
        jnp.einsum("rhd,rjhd->rhj", queries, cached_keys, preferred_element_type=jnp.float32)
        * score_scale
    )
    own_score = (
        jnp.sum(
            queries.astype(jnp.float32)
            * new_key.reshape(row_count, head_count, HD).astype(jnp.float32),
            axis=-1,
        )
        * score_scale
    )
    positions = jnp.arange(cache_len, dtype=jnp.int32)
    is_valid = positions[None, None, :] < lengths[:, None, None]
    scores = jnp.where(is_valid, scores, -jnp.inf)
    highest = jnp.maximum(jnp.max(scores, axis=-1), own_score)
    cached_exp = jnp.exp(scores - highest[..., None])
    own_exp = jnp.exp(own_score - highest)
    denominator = jnp.sum(cached_exp, axis=-1) + own_exp
    cached_prob = (cached_exp / denominator[..., None]).astype(jnp.bfloat16)
    own_prob = (own_exp / denominator).astype(jnp.bfloat16)
    mixed_values = jnp.einsum(
        "rhj,rjhd->rhd", cached_prob, cached_values, preferred_element_type=jnp.float32
    )
    mixed_values = mixed_values + own_prob.astype(jnp.float32)[..., None] * new_value.reshape(
        row_count, head_count, HD
    ).astype(jnp.float32)
    return mixed_values.reshape(row_count, local_width).astype(jnp.bfloat16)


def slot_tables(block_ids, block_weights, capacity):
    blocks, rows, picks = block_ids.shape
    expert_hit = block_ids[..., None] == jnp.arange(EXPERTS, dtype=jnp.int32)
    flat_hits = expert_hit.reshape(blocks, rows * picks, EXPERTS).astype(jnp.int32)
    earlier = jnp.cumsum(flat_hits, axis=1) - flat_hits
    slot_index = jnp.sum(earlier * flat_hits, axis=-1).reshape(blocks, rows, picks)
    slot_hit = slot_index[..., None] == jnp.arange(capacity, dtype=jnp.int32)
    pair_hit = expert_hit[..., :, None] & slot_hit[..., None, :]
    selector = jnp.any(pair_hit, axis=2).astype(jnp.bfloat16)
    combiner = jnp.sum(jnp.where(pair_hit, block_weights[..., None, None], 0.0), axis=2)
    return (selector, combiner)


def shards(
    query,
    new_key,
    new_value,
    key_cache,
    value_cache,
    lengths,
    resid,
    out_weight,
    norm_gain,
    expert_ids,
    route_weight,
    gate_weight,
    up_weight,
    down_weight,
):
    row_count = query.shape[0]
    attn_out = local_attention(query, new_key, new_value, key_cache, value_cache, lengths)
    model_width = out_weight.shape[1]
    share = model_width // lax.axis_size("tp")
    col_start = lax.axis_index("tp") * share
    resid_float = resid.astype(jnp.float32)
    proj_part = jnp.dot(attn_out, out_weight, preferred_element_type=jnp.float32)
    proj_all = lax.all_gather(proj_part, "tp", axis=0, tiled=False)
    hidden_full = resid_float + jnp.sum(proj_all, axis=0)
    mean_square = jnp.mean(hidden_full * hidden_full, axis=1)
    inv_rms = lax.rsqrt(mean_square + 1e-05)
    hidden_state = lax.dynamic_slice_in_dim(hidden_full, col_start, share, 1)
    normed = (hidden_state * inv_rms[:, None] * norm_gain[None, :]).astype(jnp.bfloat16)
    req_count = lax.axis_size("req")
    group_size = req_count // EXPERTS
    capacity = max(2, row_count // 2)
    first_row = lax.axis_index("req") * row_count
    my_ids = lax.dynamic_slice_in_dim(expert_ids, first_row, row_count, 0)
    my_weights = lax.dynamic_slice_in_dim(route_weight, first_row, row_count, 0)
    selector, combiner = slot_tables(my_ids[None], my_weights[None], capacity)
    expert_rows = jnp.einsum(
        "tec,tf->ecf", selector[0], normed, preferred_element_type=jnp.float32
    ).astype(jnp.bfloat16)
    outgoing = jnp.repeat(expert_rows, group_size, axis=0)
    arrived = lax.all_to_all(outgoing, "req", split_axis=0, concat_axis=0, tiled=True)
    token_rows = arrived.reshape(req_count * capacity, share)
    gate_part = jnp.dot(token_rows, gate_weight, preferred_element_type=jnp.float32)
    up_part = jnp.dot(token_rows, up_weight, preferred_element_type=jnp.float32)
    tp_count = lax.axis_size("tp")
    slot_count = token_rows.shape[0]
    chunk = gate_part.shape[1] // tp_count
    both = jnp.stack(
        [gate_part.reshape(slot_count, tp_count, chunk), up_part.reshape(slot_count, tp_count, chunk)],
        axis=2,
    )
    both = jnp.moveaxis(both, 1, 0).astype(jnp.bfloat16)
    both = lax.all_to_all(both, "tp", split_axis=0, concat_axis=0, tiled=True)
    summed = jnp.sum(both.astype(jnp.float32), axis=0)
    activ_chunk = (jax.nn.silu(summed[:, 0]) * summed[:, 1]).astype(jnp.bfloat16)
    activ = lax.all_gather(activ_chunk, "tp", axis=1, tiled=True)
    partial_out = (
        jnp.dot(activ, down_weight, preferred_element_type=jnp.float32)
        .astype(jnp.bfloat16)
        .reshape(req_count, capacity, share)
    )
    returned = lax.all_to_all(partial_out, "req", split_axis=0, concat_axis=0, tiled=True)
    grouped = jnp.sum(
        returned.reshape(EXPERTS, group_size, capacity, share).astype(jnp.float32), axis=1
    )
    moe_sum = jnp.einsum("tec,ecf->tf", combiner[0], grouped, precision=lax.Precision.HIGHEST)
    return (hidden_state + moe_sum).astype(jnp.bfloat16)


def solution(mesh):
    placed = (
        P("req", "tp"),
        P("req", "tp"),
        P("req", "tp"),
        P("req", None, "tp"),
        P("req", None, "tp"),
        P("req"),
        P("req", None),
        P("tp", None),
        P("tp"),
        P(),
        P(),
        P("tp", "req"),
        P("tp", "req"),
        P("req", "tp"),
    )
    return jax.shard_map(
        shards, mesh=mesh, in_specs=placed, out_specs=P("req", "tp"), check_vma=False
    )
```

```python
import jax
import jax.numpy as jnp
from jax import lax
from jax.sharding import PartitionSpec as P

HD = 64
EXPERTS = 8


def local_attention(query, new_key, new_value, key_cache, value_cache, lengths):
    local_width = query.shape[1]
    head_count = local_width // HD
    cache_len = key_cache.shape[1]
    score_scale = HD ** (-0.5)
    lane_head = jnp.arange(local_width, dtype=jnp.int32) // HD
    head_mask = lane_head[None, :] == jnp.arange(head_count, dtype=jnp.int32)[:, None]
    masked_query = jnp.where(head_mask[None], query[:, None, :], jnp.zeros((), query.dtype))
    scores = (
        jnp.einsum("rhf,rjf->rhj", masked_query, key_cache, preferred_element_type=jnp.float32)
        * score_scale
    )
    own_score = (
        jnp.einsum("rhf,rf->rh", masked_query, new_key, preferred_element_type=jnp.float32)
        * score_scale
    )
    positions = jnp.arange(cache_len, dtype=jnp.int32)
    is_valid = positions[None, None, :] < lengths[:, None, None]
    scores = jnp.where(is_valid, scores, -jnp.inf)
    highest = jnp.maximum(jnp.max(scores, axis=-1), own_score)
    cached_exp = jnp.exp(scores - highest[..., None])
    own_exp = jnp.exp(own_score - highest)
    denominator = jnp.sum(cached_exp, axis=-1) + own_exp
    cached_prob = (cached_exp / denominator[..., None]).astype(jnp.bfloat16)
    own_prob = (own_exp / denominator).astype(jnp.bfloat16)
    mixed_heads = jnp.einsum(
        "rhj,rjf->rhf", cached_prob, value_cache, preferred_element_type=jnp.float32
    )
    mixed_values = jnp.sum(jnp.where(head_mask[None], mixed_heads, 0.0), axis=1)
    own_lanes = jnp.repeat(own_prob.astype(jnp.float32), HD, axis=1)
    mixed_values = mixed_values + own_lanes * new_value.astype(jnp.float32)
    return mixed_values.astype(jnp.bfloat16)


def slot_tables(block_ids, block_weights, capacity):
    blocks, rows, picks = block_ids.shape
    expert_hit = block_ids[..., None] == jnp.arange(EXPERTS, dtype=jnp.int32)
    flat_hits = expert_hit.reshape(blocks, rows * picks, EXPERTS).astype(jnp.int32)
    earlier = jnp.cumsum(flat_hits, axis=1) - flat_hits
    slot_index = jnp.sum(earlier * flat_hits, axis=-1).reshape(blocks, rows, picks)
    slot_hit = slot_index[..., None] == jnp.arange(capacity, dtype=jnp.int32)
    pair_hit = expert_hit[..., :, None] & slot_hit[..., None, :]
    selector = jnp.any(pair_hit, axis=2).astype(jnp.bfloat16)
    combiner = jnp.sum(jnp.where(pair_hit, block_weights[..., None, None], 0.0), axis=2)
    return (selector, combiner)


def shards(
    query,
    new_key,
    new_value,
    key_cache,
    value_cache,
    lengths,
    resid,
    out_weight,
    norm_gain,
    expert_ids,
    route_weight,
    gate_weight,
    up_weight,
    down_weight,
):
    row_count = query.shape[0]
    attn_out = local_attention(query, new_key, new_value, key_cache, value_cache, lengths)
    model_width = out_weight.shape[1]
    share = model_width // lax.axis_size("tp")
    col_start = lax.axis_index("tp") * share
    resid_float = resid.astype(jnp.float32)
    proj_part = jnp.dot(attn_out, out_weight, preferred_element_type=jnp.float32)
    proj_all = lax.all_gather(proj_part, "tp", axis=0, tiled=False)
    hidden_full = resid_float + jnp.sum(proj_all, axis=0)
    mean_square = jnp.mean(hidden_full * hidden_full, axis=1)
    inv_rms = lax.rsqrt(mean_square + 1e-05)
    hidden_state = lax.dynamic_slice_in_dim(hidden_full, col_start, share, 1)
    normed = (hidden_state * inv_rms[:, None] * norm_gain[None, :]).astype(jnp.bfloat16)
    req_count = lax.axis_size("req")
    group_size = req_count // EXPERTS
    capacity = max(2, row_count // 2)
    first_row = lax.axis_index("req") * row_count
    my_ids = lax.dynamic_slice_in_dim(expert_ids, first_row, row_count, 0)
    my_weights = lax.dynamic_slice_in_dim(route_weight, first_row, row_count, 0)
    selector, combiner = slot_tables(my_ids[None], my_weights[None], capacity)
    expert_rows = jnp.einsum(
        "tec,tf->ecf", selector[0], normed, preferred_element_type=jnp.float32
    ).astype(jnp.bfloat16)
    outgoing = jnp.repeat(expert_rows, group_size, axis=0)
    arrived = lax.all_to_all(outgoing, "req", split_axis=0, concat_axis=0, tiled=True)
    token_rows = arrived.reshape(req_count * capacity, share)
    gate_part = jnp.dot(token_rows, gate_weight, preferred_element_type=jnp.float32)
    up_part = jnp.dot(token_rows, up_weight, preferred_element_type=jnp.float32)
    tp_count = lax.axis_size("tp")
    slot_count = token_rows.shape[0]
    chunk = gate_part.shape[1] // tp_count
    both = jnp.stack(
        [gate_part.reshape(slot_count, tp_count, chunk), up_part.reshape(slot_count, tp_count, chunk)],
        axis=2,
    )
    both = jnp.moveaxis(both, 1, 0).astype(jnp.bfloat16)
    both = lax.all_to_all(both, "tp", split_axis=0, concat_axis=0, tiled=True)
    summed = jnp.sum(both.astype(jnp.float32), axis=0)
    activ_chunk = (jax.nn.silu(summed[:, 0]) * summed[:, 1]).astype(jnp.bfloat16)
    activ = lax.all_gather(activ_chunk, "tp", axis=1, tiled=True)
    partial_out = (
        jnp.dot(activ, down_weight, preferred_element_type=jnp.float32)
        .astype(jnp.bfloat16)
        .reshape(req_count, capacity, share)
    )
    returned = lax.all_to_all(partial_out, "req", split_axis=0, concat_axis=0, tiled=True)
    grouped = jnp.sum(
        returned.reshape(EXPERTS, group_size, capacity, share).astype(jnp.float32), axis=1
    )
    moe_sum = jnp.einsum("tec,ecf->tf", combiner[0], grouped, precision=lax.Precision.HIGHEST)
    return (hidden_state + moe_sum).astype(jnp.bfloat16)


def solution(mesh):
    placed = (
        P("req", "tp"),
        P("req", "tp"),
        P("req", "tp"),
        P("req", None, "tp"),
        P("req", None, "tp"),
        P("req"),
        P("req", None),
        P("tp", None),
        P("tp"),
        P(),
        P(),
        P("tp", "req"),
        P("tp", "req"),
        P("req", "tp"),
    )
    return jax.shard_map(
        shards, mesh=mesh, in_specs=placed, out_specs=P("req", "tp"), check_vma=False
    )
```

```python
import jax
import jax.numpy as jnp
from jax import lax
from jax.sharding import PartitionSpec as P
from jax.experimental import pallas as pl
from jax.experimental.pallas import tpu as pltpu

HD = 64
EXPERTS = 8


def attention_kernel(len_ref, q_ref, nk_ref, nv_ref, k_ref, v_ref, o_ref):
    row_count, local_width = q_ref.shape
    head_count = local_width // HD
    cache_len = k_ref.shape[2]
    score_scale = HD ** (-0.5)
    lane_head = lax.broadcasted_iota(jnp.int32, (head_count, local_width), 1) // HD
    head_mask = lane_head == lax.broadcasted_iota(jnp.int32, (head_count, local_width), 0)
    positions = lax.broadcasted_iota(jnp.int32, (head_count, cache_len), 1)
    queries = q_ref[...].astype(jnp.float32)
    new_keys = nk_ref[...].astype(jnp.float32)
    new_values = nv_ref[...].astype(jnp.float32)
    for r in range(row_count):
        query_row = queries[r : r + 1, :]
        masked_query = jnp.where(head_mask, query_row, 0.0)
        scores = (
            lax.dot_general(
                masked_query.astype(jnp.bfloat16),
                k_ref[r],
                (((1,), (0,)), ((), ())),
                preferred_element_type=jnp.float32,
            )
            * score_scale
        )
        own_score = (
            jnp.sum(masked_query * new_keys[r : r + 1, :], axis=1, keepdims=True) * score_scale
        )
        scores = jnp.where(positions < len_ref[r], scores, -jnp.inf)
        highest = jnp.maximum(jnp.max(scores, axis=1, keepdims=True), own_score)
        cached_exp = jnp.exp(scores - highest)
        own_exp = jnp.exp(own_score - highest)
        denominator = jnp.sum(cached_exp, axis=1, keepdims=True) + own_exp
        cached_prob = (cached_exp / denominator).astype(jnp.bfloat16)
        own_prob = (own_exp / denominator).astype(jnp.bfloat16).astype(jnp.float32)
        mixed_heads = lax.dot_general(
            cached_prob, v_ref[r], (((1,), (1,)), ((), ())), preferred_element_type=jnp.float32
        )
        mixed = jnp.sum(jnp.where(head_mask, mixed_heads, 0.0), axis=0, keepdims=True)
        own_lanes = jnp.sum(jnp.where(head_mask, own_prob, 0.0), axis=0, keepdims=True)
        o_ref[r : r + 1, :] = (mixed + own_lanes * new_values[r : r + 1, :]).astype(o_ref.dtype)


def local_attention(query, new_key, new_value, key_cache, value_cache, lengths):
    row_count, local_width = query.shape
    cache_len = key_cache.shape[1]
    vmem = pl.BlockSpec(memory_space=pltpu.VMEM)
    return pl.pallas_call(
        attention_kernel,
        out_shape=jax.ShapeDtypeStruct((row_count, local_width), jnp.bfloat16),
        in_specs=[pl.BlockSpec(memory_space=pltpu.SMEM)] + [vmem] * 5,
        out_specs=vmem,
        cost_estimate=pl.CostEstimate(
            flops=4 * row_count * (local_width // HD) * cache_len * local_width,
            transcendentals=row_count * (local_width // HD) * (cache_len + 1),
            bytes_accessed=2 * key_cache.size * 2 + 4 * query.size * 2,
        ),
    )(
        lengths,
        query,
        new_key,
        new_value,
        jnp.swapaxes(key_cache, 1, 2),
        jnp.swapaxes(value_cache, 1, 2),
    )


def slot_tables(block_ids, block_weights, capacity):
    blocks, rows, picks = block_ids.shape
    expert_hit = block_ids[..., None] == jnp.arange(EXPERTS, dtype=jnp.int32)
    flat_hits = expert_hit.reshape(blocks, rows * picks, EXPERTS).astype(jnp.int32)
    earlier = jnp.cumsum(flat_hits, axis=1) - flat_hits
    slot_index = jnp.sum(earlier * flat_hits, axis=-1).reshape(blocks, rows, picks)
    slot_hit = slot_index[..., None] == jnp.arange(capacity, dtype=jnp.int32)
    pair_hit = expert_hit[..., :, None] & slot_hit[..., None, :]
    selector = jnp.any(pair_hit, axis=2).astype(jnp.bfloat16)
    combiner = jnp.sum(jnp.where(pair_hit, block_weights[..., None, None], 0.0), axis=2)
    return (selector, combiner)


def shards(
    query,
    new_key,
    new_value,
    key_cache,
    value_cache,
    lengths,
    resid,
    out_weight,
    norm_gain,
    expert_ids,
    route_weight,
    gate_weight,
    up_weight,
    down_weight,
):
    row_count = query.shape[0]
    attn_out = local_attention(query, new_key, new_value, key_cache, value_cache, lengths)
    model_width = out_weight.shape[1]
    share = model_width // lax.axis_size("tp")
    col_start = lax.axis_index("tp") * share
    resid_float = resid.astype(jnp.float32)
    proj_part = jnp.dot(attn_out, out_weight, preferred_element_type=jnp.float32)
    proj_all = lax.all_gather(proj_part, "tp", axis=0, tiled=False)
    hidden_full = resid_float + jnp.sum(proj_all, axis=0)
    mean_square = jnp.mean(hidden_full * hidden_full, axis=1)
    inv_rms = lax.rsqrt(mean_square + 1e-05)
    hidden_state = lax.dynamic_slice_in_dim(hidden_full, col_start, share, 1)
    normed = (hidden_state * inv_rms[:, None] * norm_gain[None, :]).astype(jnp.bfloat16)
    req_count = lax.axis_size("req")
    group_size = req_count // EXPERTS
    capacity = max(2, row_count // 2)
    first_row = lax.axis_index("req") * row_count
    my_ids = lax.dynamic_slice_in_dim(expert_ids, first_row, row_count, 0)
    my_weights = lax.dynamic_slice_in_dim(route_weight, first_row, row_count, 0)
    selector, combiner = slot_tables(my_ids[None], my_weights[None], capacity)
    expert_rows = jnp.einsum(
        "tec,tf->ecf", selector[0], normed, preferred_element_type=jnp.float32
    ).astype(jnp.bfloat16)
    outgoing = jnp.repeat(expert_rows, group_size, axis=0)
    arrived = lax.all_to_all(outgoing, "req", split_axis=0, concat_axis=0, tiled=True)
    token_rows = arrived.reshape(req_count * capacity, share)
    gate_part = jnp.dot(token_rows, gate_weight, preferred_element_type=jnp.float32)
    up_part = jnp.dot(token_rows, up_weight, preferred_element_type=jnp.float32)
    tp_count = lax.axis_size("tp")
    slot_count = token_rows.shape[0]
    chunk = gate_part.shape[1] // tp_count
    both = jnp.stack(
        [gate_part.reshape(slot_count, tp_count, chunk), up_part.reshape(slot_count, tp_count, chunk)],
        axis=2,
    )
    both = jnp.moveaxis(both, 1, 0).astype(jnp.bfloat16)
    both = lax.all_to_all(both, "tp", split_axis=0, concat_axis=0, tiled=True)
    summed = jnp.sum(both.astype(jnp.float32), axis=0)
    activ_chunk = (jax.nn.silu(summed[:, 0]) * summed[:, 1]).astype(jnp.bfloat16)
    activ = lax.all_gather(activ_chunk, "tp", axis=1, tiled=True)
    partial_out = (
        jnp.dot(activ, down_weight, preferred_element_type=jnp.float32)
        .astype(jnp.bfloat16)
        .reshape(req_count, capacity, share)
    )
    returned = lax.all_to_all(partial_out, "req", split_axis=0, concat_axis=0, tiled=True)
    grouped = jnp.sum(
        returned.reshape(EXPERTS, group_size, capacity, share).astype(jnp.float32), axis=1
    )
    moe_sum = jnp.einsum("tec,ecf->tf", combiner[0], grouped, precision=lax.Precision.HIGHEST)
    return (hidden_state + moe_sum).astype(jnp.bfloat16)


def solution(mesh):
    placed = (
        P("req", "tp"),
        P("req", "tp"),
        P("req", "tp"),
        P("req", None, "tp"),
        P("req", None, "tp"),
        P("req"),
        P("req", None),
        P("tp", None),
        P("tp"),
        P(),
        P(),
        P("tp", "req"),
        P("tp", "req"),
        P("req", "tp"),
    )
    return jax.shard_map(
        shards, mesh=mesh, in_specs=placed, out_specs=P("req", "tp"), check_vma=False
    )
```

```python
import jax
import jax.numpy as jnp
from jax import lax
from jax.sharding import PartitionSpec as P
from jax.experimental import pallas as pl
from jax.experimental.pallas import tpu as pltpu

HD = 64
EXPERTS = 8


def attention_kernel(len_ref, q_ref, nk_ref, nv_ref, k_ref, v_ref, o_ref):
    row_count, local_width = q_ref.shape
    head_count = local_width // HD
    cache_len = k_ref.shape[2]
    score_scale = HD ** (-0.5)
    lane_head = lax.broadcasted_iota(jnp.int32, (head_count, local_width), 1) // HD
    head_mask = lane_head == lax.broadcasted_iota(jnp.int32, (head_count, local_width), 0)
    positions = lax.broadcasted_iota(jnp.int32, (head_count, cache_len), 1)
    queries = q_ref[...].astype(jnp.float32)
    new_keys = nk_ref[...].astype(jnp.float32)
    new_values = nv_ref[...].astype(jnp.float32)
    for r in range(row_count):
        query_row = queries[r : r + 1, :]
        masked_query = jnp.where(head_mask, query_row, 0.0)
        scores = (
            lax.dot_general(
                masked_query.astype(jnp.bfloat16),
                k_ref[r],
                (((1,), (0,)), ((), ())),
                preferred_element_type=jnp.float32,
            )
            * score_scale
        )
        own_score = (
            jnp.sum(masked_query * new_keys[r : r + 1, :], axis=1, keepdims=True) * score_scale
        )
        scores = jnp.where(positions < len_ref[r], scores, -jnp.inf)
        highest = jnp.maximum(jnp.max(scores, axis=1, keepdims=True), own_score)
        cached_exp = jnp.exp(scores - highest)
        own_exp = jnp.exp(own_score - highest)
        denominator = jnp.sum(cached_exp, axis=1, keepdims=True) + own_exp
        cached_prob = (cached_exp / denominator).astype(jnp.bfloat16)
        own_prob = (own_exp / denominator).astype(jnp.bfloat16).astype(jnp.float32)
        mixed_heads = lax.dot_general(
            cached_prob, v_ref[r], (((1,), (1,)), ((), ())), preferred_element_type=jnp.float32
        )
        mixed = jnp.sum(jnp.where(head_mask, mixed_heads, 0.0), axis=0, keepdims=True)
        own_lanes = jnp.sum(jnp.where(head_mask, own_prob, 0.0), axis=0, keepdims=True)
        o_ref[r : r + 1, :] = (mixed + own_lanes * new_values[r : r + 1, :]).astype(o_ref.dtype)


def local_attention(query, new_key, new_value, key_cache, value_cache, lengths):
    row_count, local_width = query.shape
    cache_len = key_cache.shape[1]
    vmem = pl.BlockSpec(memory_space=pltpu.VMEM)
    return pl.pallas_call(
        attention_kernel,
        out_shape=jax.ShapeDtypeStruct((row_count, local_width), jnp.bfloat16),
        in_specs=[pl.BlockSpec(memory_space=pltpu.SMEM)] + [vmem] * 5,
        out_specs=vmem,
        cost_estimate=pl.CostEstimate(
            flops=4 * row_count * (local_width // HD) * cache_len * local_width,
            transcendentals=row_count * (local_width // HD) * (cache_len + 1),
            bytes_accessed=2 * key_cache.size * 2 + 4 * query.size * 2,
        ),
    )(
        lengths,
        query,
        new_key,
        new_value,
        jnp.swapaxes(key_cache, 1, 2),
        jnp.swapaxes(value_cache, 1, 2),
    )


def slot_tables(block_ids, block_weights, capacity):
    blocks, rows, picks = block_ids.shape
    expert_hit = block_ids[..., None] == jnp.arange(EXPERTS, dtype=jnp.int32)
    flat_hits = expert_hit.reshape(blocks, rows * picks, EXPERTS).astype(jnp.int32)
    earlier = jnp.cumsum(flat_hits, axis=1) - flat_hits
    slot_index = jnp.sum(earlier * flat_hits, axis=-1).reshape(blocks, rows, picks)
    slot_hit = slot_index[..., None] == jnp.arange(capacity, dtype=jnp.int32)
    pair_hit = expert_hit[..., :, None] & slot_hit[..., None, :]
    selector = jnp.any(pair_hit, axis=2).astype(jnp.bfloat16)
    combiner = jnp.sum(jnp.where(pair_hit, block_weights[..., None, None], 0.0), axis=2)
    return (selector, combiner)


def shards(
    query,
    new_key,
    new_value,
    key_cache,
    value_cache,
    lengths,
    resid,
    out_weight,
    norm_gain,
    expert_ids,
    route_weight,
    gate_weight,
    up_weight,
    down_weight,
):
    row_count = query.shape[0]
    attn_out = local_attention(query, new_key, new_value, key_cache, value_cache, lengths)
    model_width = out_weight.shape[1]
    share = model_width // lax.axis_size("tp")
    col_start = lax.axis_index("tp") * share
    resid_float = resid.astype(jnp.float32)
    proj_part = jnp.dot(attn_out, out_weight, preferred_element_type=jnp.float32)
    proj_all = lax.all_gather(proj_part, "tp", axis=0, tiled=False)
    hidden_full = resid_float + jnp.sum(proj_all, axis=0)
    mean_square = jnp.mean(hidden_full * hidden_full, axis=1)
    inv_rms = lax.rsqrt(mean_square + 1e-05)
    hidden_state = lax.dynamic_slice_in_dim(hidden_full, col_start, share, 1)
    normed = (hidden_state * inv_rms[:, None] * norm_gain[None, :]).astype(jnp.bfloat16)
    req_count = lax.axis_size("req")
    group_size = req_count // EXPERTS
    capacity = max(2, row_count // 2)
    first_row = lax.axis_index("req") * row_count
    my_ids = lax.dynamic_slice_in_dim(expert_ids, first_row, row_count, 0)
    my_weights = lax.dynamic_slice_in_dim(route_weight, first_row, row_count, 0)
    selector, combiner = slot_tables(my_ids[None], my_weights[None], capacity)
    expert_rows = jnp.einsum(
        "tec,tf->ecf", selector[0], normed, preferred_element_type=jnp.float32
    ).astype(jnp.bfloat16)
    outgoing = jnp.repeat(expert_rows, group_size, axis=0)
    arrived = lax.all_to_all(outgoing, "req", split_axis=0, concat_axis=0, tiled=True)
    token_rows = arrived.reshape(req_count * capacity, share)
    tp_count = lax.axis_size("tp")
    chunk = gate_weight.shape[1] // tp_count
    paired_weight = jnp.concatenate(
        [
            gate_weight.reshape(share, tp_count, chunk),
            up_weight.reshape(share, tp_count, chunk),
        ],
        axis=2,
    )
    both = jnp.einsum(
        "sf,ftk->tsk", token_rows, paired_weight, preferred_element_type=jnp.float32
    ).astype(jnp.bfloat16)
    both = lax.all_to_all(both, "tp", split_axis=0, concat_axis=0, tiled=True)
    summed = jnp.sum(both.astype(jnp.float32), axis=0)
    summed = jnp.stack([summed[:, :chunk], summed[:, chunk:]], axis=1)
    activ_chunk = (jax.nn.silu(summed[:, 0]) * summed[:, 1]).astype(jnp.bfloat16)
    activ = lax.all_gather(activ_chunk, "tp", axis=1, tiled=True)
    partial_out = (
        jnp.dot(activ, down_weight, preferred_element_type=jnp.float32)
        .astype(jnp.bfloat16)
        .reshape(req_count, capacity, share)
    )
    returned = lax.all_to_all(partial_out, "req", split_axis=0, concat_axis=0, tiled=True)
    grouped = jnp.sum(
        returned.reshape(EXPERTS, group_size, capacity, share).astype(jnp.float32), axis=1
    )
    moe_sum = jnp.einsum("tec,ecf->tf", combiner[0], grouped, precision=lax.Precision.HIGHEST)
    return (hidden_state + moe_sum).astype(jnp.bfloat16)


def solution(mesh):
    placed = (
        P("req", "tp"),
        P("req", "tp"),
        P("req", "tp"),
        P("req", None, "tp"),
        P("req", None, "tp"),
        P("req"),
        P("req", None),
        P("tp", None),
        P("tp"),
        P(),
        P(),
        P("tp", "req"),
        P("tp", "req"),
        P("req", "tp"),
    )
    return jax.shard_map(
        shards, mesh=mesh, in_specs=placed, out_specs=P("req", "tp"), check_vma=False
    )
```

```python
import jax
import jax.numpy as jnp
from jax import lax
from jax.sharding import PartitionSpec as P
from jax.experimental import pallas as pl
from jax.experimental.pallas import tpu as pltpu

HD = 64
EXPERTS = 8


def attention_kernel(len_ref, q_ref, nk_ref, nv_ref, k_ref, v_ref, o_ref):
    row_count, local_width = q_ref.shape
    head_count = local_width // HD
    cache_len = k_ref.shape[2]
    pair_count = row_count * head_count
    score_scale = HD ** (-0.5)
    pair_row = lax.broadcasted_iota(jnp.int32, (pair_count, row_count), 0) // head_count
    pick_row = (pair_row == lax.broadcasted_iota(jnp.int32, (pair_count, row_count), 1)).astype(
        jnp.bfloat16
    )
    lane_head = lax.broadcasted_iota(jnp.int32, (pair_count, local_width), 1) // HD
    pair_head = lax.broadcasted_iota(jnp.int32, (pair_count, local_width), 0) % head_count
    head_mask = lane_head == pair_head
    query_rows = jnp.dot(pick_row, q_ref[...], preferred_element_type=jnp.float32)
    new_key_rows = jnp.dot(pick_row, nk_ref[...], preferred_element_type=jnp.float32)
    masked_query = jnp.where(head_mask, query_rows, 0.0)
    all_keys = jnp.concatenate([k_ref[r] for r in range(row_count)], axis=1)
    all_values = jnp.concatenate([v_ref[r] for r in range(row_count)], axis=1)
    scores = (
        jnp.dot(masked_query.astype(jnp.bfloat16), all_keys, preferred_element_type=jnp.float32)
        * score_scale
    )
    own_score = jnp.sum(masked_query * new_key_rows, axis=1, keepdims=True) * score_scale
    column = lax.broadcasted_iota(jnp.int32, (pair_count, row_count * cache_len), 1)
    owner = lax.broadcasted_iota(jnp.int32, (pair_count, row_count * cache_len), 0) // head_count
    row_length = jnp.zeros((pair_count, row_count * cache_len), jnp.int32)
    for r in range(row_count):
        row_length = jnp.where(owner == r, len_ref[r], row_length)
    valid = (column // cache_len == owner) & (column % cache_len < row_length)
    scores = jnp.where(valid, scores, -jnp.inf)
    highest = jnp.maximum(jnp.max(scores, axis=1, keepdims=True), own_score)
    cached_exp = jnp.exp(scores - highest)
    own_exp = jnp.exp(own_score - highest)
    denominator = jnp.sum(cached_exp, axis=1, keepdims=True) + own_exp
    cached_prob = (cached_exp / denominator).astype(jnp.bfloat16)
    own_prob = (own_exp / denominator).astype(jnp.bfloat16).astype(jnp.float32)
    mixed_heads = lax.dot_general(
        cached_prob, all_values, (((1,), (1,)), ((), ())), preferred_element_type=jnp.float32
    )
    mixed_heads = jnp.where(head_mask, mixed_heads, 0.0)
    own_lanes = jnp.where(head_mask, own_prob, 0.0)
    new_values = nv_ref[...].astype(jnp.float32)
    for r in range(row_count):
        rows = slice(r * head_count, (r + 1) * head_count)
        mixed = jnp.sum(mixed_heads[rows], axis=0, keepdims=True)
        own = jnp.sum(own_lanes[rows], axis=0, keepdims=True)
        o_ref[r : r + 1, :] = (mixed + own * new_values[r : r + 1, :]).astype(o_ref.dtype)


def local_attention(query, new_key, new_value, key_cache, value_cache, lengths):
    row_count, local_width = query.shape
    cache_len = key_cache.shape[1]
    vmem = pl.BlockSpec(memory_space=pltpu.VMEM)
    return pl.pallas_call(
        attention_kernel,
        out_shape=jax.ShapeDtypeStruct((row_count, local_width), jnp.bfloat16),
        in_specs=[pl.BlockSpec(memory_space=pltpu.SMEM)] + [vmem] * 5,
        out_specs=vmem,
        cost_estimate=pl.CostEstimate(
            flops=4 * row_count * (local_width // HD) * cache_len * local_width,
            transcendentals=row_count * (local_width // HD) * (cache_len + 1),
            bytes_accessed=2 * key_cache.size * 2 + 4 * query.size * 2,
        ),
    )(
        lengths,
        query,
        new_key,
        new_value,
        jnp.swapaxes(key_cache, 1, 2),
        jnp.swapaxes(value_cache, 1, 2),
    )


def slot_tables(block_ids, block_weights, capacity):
    blocks, rows, picks = block_ids.shape
    expert_hit = block_ids[..., None] == jnp.arange(EXPERTS, dtype=jnp.int32)
    flat_hits = expert_hit.reshape(blocks, rows * picks, EXPERTS).astype(jnp.int32)
    earlier = jnp.cumsum(flat_hits, axis=1) - flat_hits
    slot_index = jnp.sum(earlier * flat_hits, axis=-1).reshape(blocks, rows, picks)
    slot_hit = slot_index[..., None] == jnp.arange(capacity, dtype=jnp.int32)
    pair_hit = expert_hit[..., :, None] & slot_hit[..., None, :]
    selector = jnp.any(pair_hit, axis=2).astype(jnp.bfloat16)
    combiner = jnp.sum(jnp.where(pair_hit, block_weights[..., None, None], 0.0), axis=2)
    return (selector, combiner)


def shards(
    query,
    new_key,
    new_value,
    key_cache,
    value_cache,
    lengths,
    resid,
    out_weight,
    norm_gain,
    expert_ids,
    route_weight,
    gate_weight,
    up_weight,
    down_weight,
):
    row_count = query.shape[0]
    attn_out = local_attention(query, new_key, new_value, key_cache, value_cache, lengths)
    model_width = out_weight.shape[1]
    share = model_width // lax.axis_size("tp")
    col_start = lax.axis_index("tp") * share
    resid_float = resid.astype(jnp.float32)
    proj_part = jnp.dot(attn_out, out_weight, preferred_element_type=jnp.float32)
    proj_all = lax.all_gather(proj_part, "tp", axis=0, tiled=False)
    hidden_full = resid_float + jnp.sum(proj_all, axis=0)
    mean_square = jnp.mean(hidden_full * hidden_full, axis=1)
    inv_rms = lax.rsqrt(mean_square + 1e-05)
    hidden_state = lax.dynamic_slice_in_dim(hidden_full, col_start, share, 1)
    normed = (hidden_state * inv_rms[:, None] * norm_gain[None, :]).astype(jnp.bfloat16)
    req_count = lax.axis_size("req")
    group_size = req_count // EXPERTS
    capacity = max(2, row_count // 2)
    first_row = lax.axis_index("req") * row_count
    my_ids = lax.dynamic_slice_in_dim(expert_ids, first_row, row_count, 0)
    my_weights = lax.dynamic_slice_in_dim(route_weight, first_row, row_count, 0)
    selector, combiner = slot_tables(my_ids[None], my_weights[None], capacity)
    expert_rows = jnp.einsum(
        "tec,tf->ecf", selector[0], normed, preferred_element_type=jnp.float32
    ).astype(jnp.bfloat16)
    outgoing = jnp.repeat(expert_rows, group_size, axis=0)
    arrived = lax.all_to_all(outgoing, "req", split_axis=0, concat_axis=0, tiled=True)
    token_rows = arrived.reshape(req_count * capacity, share)
    tp_count = lax.axis_size("tp")
    chunk = gate_weight.shape[1] // tp_count
    paired_weight = jnp.concatenate(
        [
            gate_weight.reshape(share, tp_count, chunk),
            up_weight.reshape(share, tp_count, chunk),
        ],
        axis=2,
    )
    both = jnp.einsum(
        "sf,ftk->tsk", token_rows, paired_weight, preferred_element_type=jnp.float32
    ).astype(jnp.bfloat16)
    both = lax.all_to_all(both, "tp", split_axis=0, concat_axis=0, tiled=True)
    summed = jnp.sum(both.astype(jnp.float32), axis=0)
    summed = jnp.stack([summed[:, :chunk], summed[:, chunk:]], axis=1)
    activ_chunk = (jax.nn.silu(summed[:, 0]) * summed[:, 1]).astype(jnp.bfloat16)
    activ = lax.all_gather(activ_chunk, "tp", axis=1, tiled=True)
    partial_out = (
        jnp.dot(activ, down_weight, preferred_element_type=jnp.float32)
        .astype(jnp.bfloat16)
        .reshape(req_count, capacity, share)
    )
    returned = lax.all_to_all(partial_out, "req", split_axis=0, concat_axis=0, tiled=True)
    grouped = jnp.sum(
        returned.reshape(EXPERTS, group_size, capacity, share).astype(jnp.float32), axis=1
    )
    moe_sum = jnp.einsum("tec,ecf->tf", combiner[0], grouped, precision=lax.Precision.HIGHEST)
    return (hidden_state + moe_sum).astype(jnp.bfloat16)


def solution(mesh):
    placed = (
        P("req", "tp"),
        P("req", "tp"),
        P("req", "tp"),
        P("req", None, "tp"),
        P("req", None, "tp"),
        P("req"),
        P("req", None),
        P("tp", None),
        P("tp"),
        P(),
        P(),
        P("tp", "req"),
        P("tp", "req"),
        P("req", "tp"),
    )
    return jax.shard_map(
        shards, mesh=mesh, in_specs=placed, out_specs=P("req", "tp"), check_vma=False
    )
```

```python
import jax
import jax.numpy as jnp
from jax import lax
from jax.sharding import PartitionSpec as P
from jax.experimental import pallas as pl
from jax.experimental.pallas import tpu as pltpu

HD = 64
EXPERTS = 8


def attention_kernel(len_ref, q_ref, nk_ref, nv_ref, k_ref, v_ref, o_ref):
    row_count, local_width = q_ref.shape
    head_count = local_width // HD
    cache_len = k_ref.shape[2]
    pair_count = row_count * head_count
    score_scale = HD ** (-0.5)
    pair_row = lax.broadcasted_iota(jnp.int32, (pair_count, row_count), 0) // head_count
    pick_row = (pair_row == lax.broadcasted_iota(jnp.int32, (pair_count, row_count), 1)).astype(
        jnp.bfloat16
    )
    lane_head = lax.broadcasted_iota(jnp.int32, (pair_count, local_width), 1) // HD
    pair_head = lax.broadcasted_iota(jnp.int32, (pair_count, local_width), 0) % head_count
    head_mask = lane_head == pair_head
    query_rows = jnp.dot(pick_row, q_ref[...], preferred_element_type=jnp.float32)
    new_key_rows = jnp.dot(pick_row, nk_ref[...], preferred_element_type=jnp.float32)
    masked_query = jnp.where(head_mask, query_rows, 0.0)
    all_keys = jnp.concatenate([k_ref[r] for r in range(row_count)], axis=1)
    all_values = jnp.concatenate([v_ref[r] for r in range(row_count)], axis=1)
    scores = (
        jnp.dot(masked_query.astype(jnp.bfloat16), all_keys, preferred_element_type=jnp.float32)
        * score_scale
    )
    own_score = jnp.sum(masked_query * new_key_rows, axis=1, keepdims=True) * score_scale
    column = lax.broadcasted_iota(jnp.int32, (pair_count, row_count * cache_len), 1)
    owner = lax.broadcasted_iota(jnp.int32, (pair_count, row_count * cache_len), 0) // head_count
    row_length = jnp.zeros((pair_count, row_count * cache_len), jnp.int32)
    for r in range(row_count):
        row_length = jnp.where(owner == r, len_ref[r], row_length)
    valid = (column // cache_len == owner) & (column % cache_len < row_length)
    scores = jnp.where(valid, scores, -jnp.inf)
    highest = jnp.maximum(jnp.max(scores, axis=1, keepdims=True), own_score)
    cached_exp = jnp.exp(scores - highest)
    own_exp = jnp.exp(own_score - highest)
    denominator = jnp.sum(cached_exp, axis=1, keepdims=True) + own_exp
    cached_prob = (cached_exp / denominator).astype(jnp.bfloat16)
    own_prob = (own_exp / denominator).astype(jnp.bfloat16).astype(jnp.float32)
    mixed_heads = lax.dot_general(
        cached_prob, all_values, (((1,), (1,)), ((), ())), preferred_element_type=jnp.float32
    )
    mixed_heads = jnp.where(head_mask, mixed_heads, 0.0)
    own_lanes = jnp.where(head_mask, own_prob, 0.0)
    new_values = nv_ref[...].astype(jnp.float32)
    for r in range(row_count):
        rows = slice(r * head_count, (r + 1) * head_count)
        mixed = jnp.sum(mixed_heads[rows], axis=0, keepdims=True)
        own = jnp.sum(own_lanes[rows], axis=0, keepdims=True)
        o_ref[r : r + 1, :] = (mixed + own * new_values[r : r + 1, :]).astype(o_ref.dtype)


def local_attention(query, new_key, new_value, key_cache, value_cache, lengths):
    row_count, local_width = query.shape
    cache_len = key_cache.shape[1]
    vmem = pl.BlockSpec(memory_space=pltpu.VMEM)
    return pl.pallas_call(
        attention_kernel,
        out_shape=jax.ShapeDtypeStruct((row_count, local_width), jnp.bfloat16),
        in_specs=[pl.BlockSpec(memory_space=pltpu.SMEM)] + [vmem] * 5,
        out_specs=vmem,
        cost_estimate=pl.CostEstimate(
            flops=4 * row_count * (local_width // HD) * cache_len * local_width,
            transcendentals=row_count * (local_width // HD) * (cache_len + 1),
            bytes_accessed=2 * key_cache.size * 2 + 4 * query.size * 2,
        ),
    )(
        lengths,
        query,
        new_key,
        new_value,
        jnp.swapaxes(key_cache, 1, 2),
        jnp.swapaxes(value_cache, 1, 2),
    )


def slot_tables(block_ids, block_weights, capacity):
    blocks, rows, picks = block_ids.shape
    expert_hit = block_ids[..., None] == jnp.arange(EXPERTS, dtype=jnp.int32)
    flat_hits = expert_hit.reshape(blocks, rows * picks, EXPERTS).astype(jnp.int32)
    earlier = jnp.cumsum(flat_hits, axis=1) - flat_hits
    slot_index = jnp.sum(earlier * flat_hits, axis=-1).reshape(blocks, rows, picks)
    slot_hit = slot_index[..., None] == jnp.arange(capacity, dtype=jnp.int32)
    pair_hit = expert_hit[..., :, None] & slot_hit[..., None, :]
    selector = jnp.any(pair_hit, axis=2).astype(jnp.bfloat16)
    combiner = jnp.sum(jnp.where(pair_hit, block_weights[..., None, None], 0.0), axis=2)
    return (selector, combiner)


def shards(
    query,
    new_key,
    new_value,
    key_cache,
    value_cache,
    lengths,
    resid,
    out_weight,
    norm_gain,
    expert_ids,
    route_weight,
    gate_weight,
    up_weight,
    down_weight,
):
    row_count = query.shape[0]
    attn_out = local_attention(query, new_key, new_value, key_cache, value_cache, lengths)
    model_width = out_weight.shape[1]
    share = model_width // lax.axis_size("tp")
    col_start = lax.axis_index("tp") * share
    resid_float = resid.astype(jnp.float32)
    proj_part = jnp.dot(attn_out, out_weight, preferred_element_type=jnp.float32)
    proj_all = lax.all_gather(proj_part, "tp", axis=0, tiled=False)
    hidden_full = resid_float + jnp.sum(proj_all, axis=0)
    mean_square = jnp.mean(hidden_full * hidden_full, axis=1)
    inv_rms = lax.rsqrt(mean_square + 1e-05)
    hidden_state = lax.dynamic_slice_in_dim(hidden_full, col_start, share, 1)
    normed = (hidden_state * inv_rms[:, None] * norm_gain[None, :]).astype(jnp.bfloat16)
    req_count = lax.axis_size("req")
    group_size = req_count // EXPERTS
    capacity = max(2, row_count // 2)
    first_row = lax.axis_index("req") * row_count
    my_ids = lax.dynamic_slice_in_dim(expert_ids, first_row, row_count, 0)
    my_weights = lax.dynamic_slice_in_dim(route_weight, first_row, row_count, 0)
    selector, combiner = slot_tables(my_ids[None], my_weights[None], capacity)
    expert_rows = jnp.einsum(
        "tec,tf->ecf", selector[0], normed, preferred_element_type=jnp.float32
    ).astype(jnp.bfloat16)
    outgoing = jnp.repeat(expert_rows, group_size, axis=0)
    arrived = lax.all_to_all(outgoing, "req", split_axis=0, concat_axis=0, tiled=True)
    token_rows = arrived.reshape(req_count * capacity, share)
    tp_count = lax.axis_size("tp")
    paired_weight = jnp.concatenate([gate_weight, up_weight], axis=1)
    both = jnp.dot(token_rows, paired_weight, preferred_element_type=jnp.float32).astype(
        jnp.bfloat16
    )
    both = jnp.broadcast_to(both[None], (tp_count,) + both.shape)
    both = lax.all_to_all(both, "tp", split_axis=0, concat_axis=0, tiled=True)
    summed = jnp.sum(both.astype(jnp.float32), axis=0)
    hidden_units = gate_weight.shape[1]
    activ = (jax.nn.silu(summed[:, :hidden_units]) * summed[:, hidden_units:]).astype(jnp.bfloat16)
    partial_out = (
        jnp.dot(activ, down_weight, preferred_element_type=jnp.float32)
        .astype(jnp.bfloat16)
        .reshape(req_count, capacity, share)
    )
    returned = lax.all_to_all(partial_out, "req", split_axis=0, concat_axis=0, tiled=True)
    grouped = jnp.sum(
        returned.reshape(EXPERTS, group_size, capacity, share).astype(jnp.float32), axis=1
    )
    moe_sum = jnp.einsum("tec,ecf->tf", combiner[0], grouped, precision=lax.Precision.HIGHEST)
    return (hidden_state + moe_sum).astype(jnp.bfloat16)


def solution(mesh):
    placed = (
        P("req", "tp"),
        P("req", "tp"),
        P("req", "tp"),
        P("req", None, "tp"),
        P("req", None, "tp"),
        P("req"),
        P("req", None),
        P("tp", None),
        P("tp"),
        P(),
        P(),
        P("tp", "req"),
        P("tp", "req"),
        P("req", "tp"),
    )
    return jax.shard_map(
        shards, mesh=mesh, in_specs=placed, out_specs=P("req", "tp"), check_vma=False
    )
```

```python
import jax
import jax.numpy as jnp
from jax import lax
from jax.sharding import PartitionSpec as P
from jax.experimental import pallas as pl
from jax.experimental.pallas import tpu as pltpu

HD = 64
EXPERTS = 8


def attention_kernel(len_ref, q_ref, nk_ref, nv_ref, k_ref, v_ref, w_hbm, o_ref, attn_ref, w_ref, w_sem):
    weight_copy = pltpu.make_async_copy(w_hbm, w_ref, w_sem)
    weight_copy.start()
    row_count, local_width = q_ref.shape
    head_count = local_width // HD
    cache_len = k_ref.shape[2]
    pair_count = row_count * head_count
    score_scale = HD ** (-0.5)
    pair_row = lax.broadcasted_iota(jnp.int32, (pair_count, row_count), 0) // head_count
    pick_row = (pair_row == lax.broadcasted_iota(jnp.int32, (pair_count, row_count), 1)).astype(
        jnp.bfloat16
    )
    lane_head = lax.broadcasted_iota(jnp.int32, (pair_count, local_width), 1) // HD
    pair_head = lax.broadcasted_iota(jnp.int32, (pair_count, local_width), 0) % head_count
    head_mask = lane_head == pair_head
    query_rows = jnp.dot(pick_row, q_ref[...], preferred_element_type=jnp.float32)
    new_key_rows = jnp.dot(pick_row, nk_ref[...], preferred_element_type=jnp.float32)
    masked_query = jnp.where(head_mask, query_rows, 0.0)
    all_keys = jnp.concatenate([k_ref[r] for r in range(row_count)], axis=1)
    all_values = jnp.concatenate([v_ref[r] for r in range(row_count)], axis=1)
    scores = (
        jnp.dot(masked_query.astype(jnp.bfloat16), all_keys, preferred_element_type=jnp.float32)
        * score_scale
    )
    own_score = jnp.sum(masked_query * new_key_rows, axis=1, keepdims=True) * score_scale
    column = lax.broadcasted_iota(jnp.int32, (pair_count, row_count * cache_len), 1)
    owner = lax.broadcasted_iota(jnp.int32, (pair_count, row_count * cache_len), 0) // head_count
    row_length = jnp.zeros((pair_count, row_count * cache_len), jnp.int32)
    for r in range(row_count):
        row_length = jnp.where(owner == r, len_ref[r], row_length)
    valid = (column // cache_len == owner) & (column % cache_len < row_length)
    scores = jnp.where(valid, scores, -jnp.inf)
    highest = jnp.maximum(jnp.max(scores, axis=1, keepdims=True), own_score)
    cached_exp = jnp.exp(scores - highest)
    own_exp = jnp.exp(own_score - highest)
    denominator = jnp.sum(cached_exp, axis=1, keepdims=True) + own_exp
    cached_prob = (cached_exp / denominator).astype(jnp.bfloat16)
    own_prob = (own_exp / denominator).astype(jnp.bfloat16).astype(jnp.float32)
    mixed_heads = lax.dot_general(
        cached_prob, all_values, (((1,), (1,)), ((), ())), preferred_element_type=jnp.float32
    )
    mixed_heads = jnp.where(head_mask, mixed_heads, 0.0)
    own_lanes = jnp.where(head_mask, own_prob, 0.0)
    new_values = nv_ref[...].astype(jnp.float32)
    for r in range(row_count):
        rows = slice(r * head_count, (r + 1) * head_count)
        mixed = jnp.sum(mixed_heads[rows], axis=0, keepdims=True)
        own = jnp.sum(own_lanes[rows], axis=0, keepdims=True)
        attn_ref[r : r + 1, :] = (mixed + own * new_values[r : r + 1, :]).astype(attn_ref.dtype)
    weight_copy.wait()
    o_ref[...] = jnp.dot(attn_ref[...], w_ref[...], preferred_element_type=jnp.float32)


def local_attention(query, new_key, new_value, key_cache, value_cache, lengths, out_weight):
    row_count, local_width = query.shape
    cache_len = key_cache.shape[1]
    vmem = pl.BlockSpec(memory_space=pltpu.VMEM)
    return pl.pallas_call(
        attention_kernel,
        out_shape=jax.ShapeDtypeStruct((row_count, out_weight.shape[1]), jnp.float32),
        in_specs=[pl.BlockSpec(memory_space=pltpu.SMEM)] + [vmem] * 5 + [pl.BlockSpec(memory_space=pl.ANY)],
        out_specs=vmem,
        scratch_shapes=[
            pltpu.VMEM((row_count, local_width), jnp.bfloat16),
            pltpu.VMEM(out_weight.shape, out_weight.dtype),
            pltpu.SemaphoreType.DMA(()),
        ],
        cost_estimate=pl.CostEstimate(
            flops=4 * row_count * (local_width // HD) * cache_len * local_width,
            transcendentals=row_count * (local_width // HD) * (cache_len + 1),
            bytes_accessed=2 * key_cache.size * 2 + 4 * query.size * 2 + out_weight.size * 2,
        ),
    )(
        lengths,
        query,
        new_key,
        new_value,
        jnp.swapaxes(key_cache, 1, 2),
        jnp.swapaxes(value_cache, 1, 2),
        out_weight,
    )


def slot_tables(block_ids, block_weights, capacity):
    blocks, rows, picks = block_ids.shape
    expert_hit = block_ids[..., None] == jnp.arange(EXPERTS, dtype=jnp.int32)
    flat_hits = expert_hit.reshape(blocks, rows * picks, EXPERTS).astype(jnp.int32)
    earlier = jnp.cumsum(flat_hits, axis=1) - flat_hits
    slot_index = jnp.sum(earlier * flat_hits, axis=-1).reshape(blocks, rows, picks)
    slot_hit = slot_index[..., None] == jnp.arange(capacity, dtype=jnp.int32)
    pair_hit = expert_hit[..., :, None] & slot_hit[..., None, :]
    selector = jnp.any(pair_hit, axis=2).astype(jnp.bfloat16)
    combiner = jnp.sum(jnp.where(pair_hit, block_weights[..., None, None], 0.0), axis=2)
    return (selector, combiner)


def shards(
    query,
    new_key,
    new_value,
    key_cache,
    value_cache,
    lengths,
    resid,
    out_weight,
    norm_gain,
    expert_ids,
    route_weight,
    gate_weight,
    up_weight,
    down_weight,
):
    row_count = query.shape[0]
    proj_part = local_attention(
        query, new_key, new_value, key_cache, value_cache, lengths, out_weight
    )
    model_width = out_weight.shape[1]
    share = model_width // lax.axis_size("tp")
    col_start = lax.axis_index("tp") * share
    resid_float = resid.astype(jnp.float32)
    proj_all = lax.all_gather(proj_part, "tp", axis=0, tiled=False)
    hidden_full = resid_float + jnp.sum(proj_all, axis=0)
    mean_square = jnp.mean(hidden_full * hidden_full, axis=1)
    inv_rms = lax.rsqrt(mean_square + 1e-05)
    hidden_state = lax.dynamic_slice_in_dim(hidden_full, col_start, share, 1)
    normed = (hidden_state * inv_rms[:, None] * norm_gain[None, :]).astype(jnp.bfloat16)
    req_count = lax.axis_size("req")
    group_size = req_count // EXPERTS
    capacity = max(2, row_count // 2)
    first_row = lax.axis_index("req") * row_count
    my_ids = lax.dynamic_slice_in_dim(expert_ids, first_row, row_count, 0)
    my_weights = lax.dynamic_slice_in_dim(route_weight, first_row, row_count, 0)
    selector, combiner = slot_tables(my_ids[None], my_weights[None], capacity)
    expert_rows = jnp.einsum(
        "tec,tf->ecf", selector[0], normed, preferred_element_type=jnp.float32
    ).astype(jnp.bfloat16)
    outgoing = jnp.repeat(expert_rows, group_size, axis=0)
    arrived = lax.all_to_all(outgoing, "req", split_axis=0, concat_axis=0, tiled=True)
    token_rows = arrived.reshape(req_count * capacity, share)
    tp_count = lax.axis_size("tp")
    paired_weight = jnp.concatenate([gate_weight, up_weight], axis=1)
    both = jnp.dot(token_rows, paired_weight, preferred_element_type=jnp.float32).astype(
        jnp.bfloat16
    )
    both = jnp.broadcast_to(both[None], (tp_count,) + both.shape)
    both = lax.all_to_all(both, "tp", split_axis=0, concat_axis=0, tiled=True)
    summed = jnp.sum(both.astype(jnp.float32), axis=0)
    hidden_units = gate_weight.shape[1]
    activ = (jax.nn.silu(summed[:, :hidden_units]) * summed[:, hidden_units:]).astype(jnp.bfloat16)
    partial_out = (
        jnp.dot(activ, down_weight, preferred_element_type=jnp.float32)
        .astype(jnp.bfloat16)
        .reshape(req_count, capacity, share)
    )
    returned = lax.all_to_all(partial_out, "req", split_axis=0, concat_axis=0, tiled=True)
    grouped = jnp.sum(
        returned.reshape(EXPERTS, group_size, capacity, share).astype(jnp.float32), axis=1
    )
    moe_sum = jnp.einsum("tec,ecf->tf", combiner[0], grouped, precision=lax.Precision.HIGHEST)
    return (hidden_state + moe_sum).astype(jnp.bfloat16)


def solution(mesh):
    placed = (
        P("req", "tp"),
        P("req", "tp"),
        P("req", "tp"),
        P("req", None, "tp"),
        P("req", None, "tp"),
        P("req"),
        P("req", None),
        P("tp", None),
        P("tp"),
        P(),
        P(),
        P("tp", "req"),
        P("tp", "req"),
        P("req", "tp"),
    )
    return jax.shard_map(
        shards, mesh=mesh, in_specs=placed, out_specs=P("req", "tp"), check_vma=False
    )
```

```python
import jax
import jax.numpy as jnp
from jax import lax
from jax.sharding import PartitionSpec as P
from jax.experimental import pallas as pl
from jax.experimental.pallas import tpu as pltpu

HD = 64
EXPERTS = 8


def attention_kernel(len_ref, q_ref, nk_ref, nv_ref, k_ref, v_ref, w_hbm, o_ref, attn_ref, w_ref, w_sem):
    pieces = w_sem.shape[0]
    piece = w_ref.shape[0] // pieces
    weight_copies = [
        pltpu.make_async_copy(
            w_hbm.at[pl.ds(p * piece, piece)], w_ref.at[pl.ds(p * piece, piece)], w_sem.at[p]
        )
        for p in range(pieces)
    ]
    for weight_copy in weight_copies:
        weight_copy.start()
    row_count, local_width = q_ref.shape
    head_count = local_width // HD
    cache_len = k_ref.shape[2]
    pair_count = row_count * head_count
    score_scale = HD ** (-0.5)
    pair_row = lax.broadcasted_iota(jnp.int32, (pair_count, row_count), 0) // head_count
    pick_row = (pair_row == lax.broadcasted_iota(jnp.int32, (pair_count, row_count), 1)).astype(
        jnp.bfloat16
    )
    lane_head = lax.broadcasted_iota(jnp.int32, (pair_count, local_width), 1) // HD
    pair_head = lax.broadcasted_iota(jnp.int32, (pair_count, local_width), 0) % head_count
    head_mask = lane_head == pair_head
    query_rows = jnp.dot(pick_row, q_ref[...], preferred_element_type=jnp.float32)
    new_key_rows = jnp.dot(pick_row, nk_ref[...], preferred_element_type=jnp.float32)
    masked_query = jnp.where(head_mask, query_rows, 0.0)
    all_keys = jnp.concatenate([k_ref[r] for r in range(row_count)], axis=1)
    all_values = jnp.concatenate([v_ref[r] for r in range(row_count)], axis=1)
    scores = (
        jnp.dot(masked_query.astype(jnp.bfloat16), all_keys, preferred_element_type=jnp.float32)
        * score_scale
    )
    own_score = jnp.sum(masked_query * new_key_rows, axis=1, keepdims=True) * score_scale
    column = lax.broadcasted_iota(jnp.int32, (pair_count, row_count * cache_len), 1)
    owner = lax.broadcasted_iota(jnp.int32, (pair_count, row_count * cache_len), 0) // head_count
    row_length = jnp.zeros((pair_count, row_count * cache_len), jnp.int32)
    for r in range(row_count):
        row_length = jnp.where(owner == r, len_ref[r], row_length)
    valid = (column // cache_len == owner) & (column % cache_len < row_length)
    scores = jnp.where(valid, scores, -jnp.inf)
    highest = jnp.maximum(jnp.max(scores, axis=1, keepdims=True), own_score)
    cached_exp = jnp.exp(scores - highest)
    own_exp = jnp.exp(own_score - highest)
    denominator = jnp.sum(cached_exp, axis=1, keepdims=True) + own_exp
    cached_prob = (cached_exp / denominator).astype(jnp.bfloat16)
    own_prob = (own_exp / denominator).astype(jnp.bfloat16).astype(jnp.float32)
    mixed_heads = lax.dot_general(
        cached_prob, all_values, (((1,), (1,)), ((), ())), preferred_element_type=jnp.float32
    )
    mixed_heads = jnp.where(head_mask, mixed_heads, 0.0)
    own_lanes = jnp.where(head_mask, own_prob, 0.0)
    new_values = nv_ref[...].astype(jnp.float32)
    for r in range(row_count):
        rows = slice(r * head_count, (r + 1) * head_count)
        mixed = jnp.sum(mixed_heads[rows], axis=0, keepdims=True)
        own = jnp.sum(own_lanes[rows], axis=0, keepdims=True)
        attn_ref[r : r + 1, :] = (mixed + own * new_values[r : r + 1, :]).astype(attn_ref.dtype)
    attn = attn_ref[...]
    total = None
    for p, weight_copy in enumerate(weight_copies):
        weight_copy.wait()
        part = jnp.dot(
            attn[:, p * piece : (p + 1) * piece],
            w_ref[p * piece : (p + 1) * piece, :],
            preferred_element_type=jnp.float32,
        )
        total = part if total is None else total + part
    o_ref[...] = total


def local_attention(query, new_key, new_value, key_cache, value_cache, lengths, out_weight):
    row_count, local_width = query.shape
    cache_len = key_cache.shape[1]
    vmem = pl.BlockSpec(memory_space=pltpu.VMEM)
    return pl.pallas_call(
        attention_kernel,
        out_shape=jax.ShapeDtypeStruct((row_count, out_weight.shape[1]), jnp.float32),
        in_specs=[pl.BlockSpec(memory_space=pltpu.SMEM)] + [vmem] * 5 + [pl.BlockSpec(memory_space=pl.ANY)],
        out_specs=vmem,
        scratch_shapes=[
            pltpu.VMEM((row_count, local_width), jnp.bfloat16),
            pltpu.VMEM(out_weight.shape, out_weight.dtype),
            pltpu.SemaphoreType.DMA((4,)),
        ],
        cost_estimate=pl.CostEstimate(
            flops=4 * row_count * (local_width // HD) * cache_len * local_width,
            transcendentals=row_count * (local_width // HD) * (cache_len + 1),
            bytes_accessed=2 * key_cache.size * 2 + 4 * query.size * 2 + out_weight.size * 2,
        ),
    )(
        lengths,
        query,
        new_key,
        new_value,
        jnp.swapaxes(key_cache, 1, 2),
        jnp.swapaxes(value_cache, 1, 2),
        out_weight,
    )


def slot_tables(block_ids, block_weights, capacity):
    blocks, rows, picks = block_ids.shape
    expert_hit = block_ids[..., None] == jnp.arange(EXPERTS, dtype=jnp.int32)
    flat_hits = expert_hit.reshape(blocks, rows * picks, EXPERTS).astype(jnp.int32)
    earlier = jnp.cumsum(flat_hits, axis=1) - flat_hits
    slot_index = jnp.sum(earlier * flat_hits, axis=-1).reshape(blocks, rows, picks)
    slot_hit = slot_index[..., None] == jnp.arange(capacity, dtype=jnp.int32)
    pair_hit = expert_hit[..., :, None] & slot_hit[..., None, :]
    selector = jnp.any(pair_hit, axis=2).astype(jnp.bfloat16)
    combiner = jnp.sum(jnp.where(pair_hit, block_weights[..., None, None], 0.0), axis=2)
    return (selector, combiner)


def shards(
    query,
    new_key,
    new_value,
    key_cache,
    value_cache,
    lengths,
    resid,
    out_weight,
    norm_gain,
    expert_ids,
    route_weight,
    gate_weight,
    up_weight,
    down_weight,
):
    row_count = query.shape[0]
    proj_part = local_attention(
        query, new_key, new_value, key_cache, value_cache, lengths, out_weight
    )
    model_width = out_weight.shape[1]
    share = model_width // lax.axis_size("tp")
    col_start = lax.axis_index("tp") * share
    resid_float = resid.astype(jnp.float32)
    proj_all = lax.all_gather(proj_part, "tp", axis=0, tiled=False)
    hidden_full = resid_float + jnp.sum(proj_all, axis=0)
    mean_square = jnp.mean(hidden_full * hidden_full, axis=1)
    inv_rms = lax.rsqrt(mean_square + 1e-05)
    hidden_state = lax.dynamic_slice_in_dim(hidden_full, col_start, share, 1)
    normed = (hidden_state * inv_rms[:, None] * norm_gain[None, :]).astype(jnp.bfloat16)
    req_count = lax.axis_size("req")
    group_size = req_count // EXPERTS
    capacity = max(2, row_count // 2)
    first_row = lax.axis_index("req") * row_count
    my_ids = lax.dynamic_slice_in_dim(expert_ids, first_row, row_count, 0)
    my_weights = lax.dynamic_slice_in_dim(route_weight, first_row, row_count, 0)
    selector, combiner = slot_tables(my_ids[None], my_weights[None], capacity)
    expert_rows = jnp.einsum(
        "tec,tf->ecf", selector[0], normed, preferred_element_type=jnp.float32
    ).astype(jnp.bfloat16)
    outgoing = jnp.repeat(expert_rows, group_size, axis=0)
    arrived = lax.all_to_all(outgoing, "req", split_axis=0, concat_axis=0, tiled=True)
    token_rows = arrived.reshape(req_count * capacity, share)
    tp_count = lax.axis_size("tp")
    paired_weight = jnp.concatenate([gate_weight, up_weight], axis=1)
    both = jnp.dot(token_rows, paired_weight, preferred_element_type=jnp.float32).astype(
        jnp.bfloat16
    )
    both = jnp.broadcast_to(both[None], (tp_count,) + both.shape)
    both = lax.all_to_all(both, "tp", split_axis=0, concat_axis=0, tiled=True)
    summed = jnp.sum(both.astype(jnp.float32), axis=0)
    hidden_units = gate_weight.shape[1]
    activ = (jax.nn.silu(summed[:, :hidden_units]) * summed[:, hidden_units:]).astype(jnp.bfloat16)
    partial_out = (
        jnp.dot(activ, down_weight, preferred_element_type=jnp.float32)
        .astype(jnp.bfloat16)
        .reshape(req_count, capacity, share)
    )
    returned = lax.all_to_all(partial_out, "req", split_axis=0, concat_axis=0, tiled=True)
    grouped = jnp.sum(
        returned.reshape(EXPERTS, group_size, capacity, share).astype(jnp.float32), axis=1
    )
    moe_sum = jnp.einsum("tec,ecf->tf", combiner[0], grouped, precision=lax.Precision.HIGHEST)
    return (hidden_state + moe_sum).astype(jnp.bfloat16)


def solution(mesh):
    placed = (
        P("req", "tp"),
        P("req", "tp"),
        P("req", "tp"),
        P("req", None, "tp"),
        P("req", None, "tp"),
        P("req"),
        P("req", None),
        P("tp", None),
        P("tp"),
        P(),
        P(),
        P("tp", "req"),
        P("tp", "req"),
        P("req", "tp"),
    )
    return jax.shard_map(
        shards, mesh=mesh, in_specs=placed, out_specs=P("req", "tp"), check_vma=False
    )
```

```python
import jax
import jax.numpy as jnp
from jax import lax
from jax.sharding import PartitionSpec as P
from jax.experimental import pallas as pl
from jax.experimental.pallas import tpu as pltpu

HD = 64
EXPERTS = 8


def attention_kernel(len_ref, q_ref, nk_ref, nv_ref, k_ref, v_ref, w_hbm, o_ref, attn_ref, w_ref, w_sem):
    pieces = w_sem.shape[0]
    piece = w_ref.shape[0] // pieces
    weight_copies = [
        pltpu.make_async_copy(
            w_hbm.at[pl.ds(p * piece, piece)], w_ref.at[pl.ds(p * piece, piece)], w_sem.at[p]
        )
        for p in range(pieces)
    ]
    for weight_copy in weight_copies:
        weight_copy.start()
    row_count, local_width = q_ref.shape
    head_count = local_width // HD
    cache_len = k_ref.shape[2]
    pair_count = row_count * head_count
    score_scale = HD ** (-0.5)
    pair_row = lax.broadcasted_iota(jnp.int32, (pair_count, row_count), 0) // head_count
    pick_row = (pair_row == lax.broadcasted_iota(jnp.int32, (pair_count, row_count), 1)).astype(
        jnp.bfloat16
    )
    lane_head = lax.broadcasted_iota(jnp.int32, (pair_count, local_width), 1) // HD
    pair_head = lax.broadcasted_iota(jnp.int32, (pair_count, local_width), 0) % head_count
    head_mask = lane_head == pair_head
    query_rows = jnp.dot(pick_row, q_ref[...], preferred_element_type=jnp.float32)
    new_key_rows = jnp.dot(pick_row, nk_ref[...], preferred_element_type=jnp.float32)
    masked_query = jnp.where(head_mask, query_rows, 0.0)
    all_keys = jnp.concatenate([k_ref[r] for r in range(row_count)], axis=1)
    all_values = jnp.concatenate([v_ref[r] for r in range(row_count)], axis=1)
    scores = (
        jnp.dot(masked_query.astype(jnp.bfloat16), all_keys, preferred_element_type=jnp.float32)
        * score_scale
    )
    own_score = jnp.sum(masked_query * new_key_rows, axis=1, keepdims=True) * score_scale
    column = lax.broadcasted_iota(jnp.int32, (pair_count, row_count * cache_len), 1)
    owner = lax.broadcasted_iota(jnp.int32, (pair_count, row_count * cache_len), 0) // head_count
    row_length = jnp.zeros((pair_count, row_count * cache_len), jnp.int32)
    for r in range(row_count):
        row_length = jnp.where(owner == r, len_ref[r], row_length)
    valid = (column // cache_len == owner) & (column % cache_len < row_length)
    scores = jnp.where(valid, scores, -jnp.inf)
    highest = jnp.maximum(jnp.max(scores, axis=1, keepdims=True), own_score)
    cached_exp = jnp.exp(scores - highest)
    own_exp = jnp.exp(own_score - highest)
    denominator = jnp.sum(cached_exp, axis=1, keepdims=True) + own_exp
    cached_prob = (cached_exp / denominator).astype(jnp.bfloat16)
    own_prob = (own_exp / denominator).astype(jnp.bfloat16).astype(jnp.float32)
    mixed_heads = lax.dot_general(
        cached_prob, all_values, (((1,), (1,)), ((), ())), preferred_element_type=jnp.float32
    )
    mixed_heads = jnp.where(head_mask, mixed_heads, 0.0)
    own_lanes = jnp.where(head_mask, own_prob, 0.0)
    new_values = nv_ref[...].astype(jnp.float32)
    for r in range(row_count):
        rows = slice(r * head_count, (r + 1) * head_count)
        mixed = jnp.sum(mixed_heads[rows], axis=0, keepdims=True)
        own = jnp.sum(own_lanes[rows], axis=0, keepdims=True)
        attn_ref[r : r + 1, :] = (mixed + own * new_values[r : r + 1, :]).astype(attn_ref.dtype)
    attn = attn_ref[...]
    total = None
    for p, weight_copy in enumerate(weight_copies):
        weight_copy.wait()
        part = jnp.dot(
            attn[:, p * piece : (p + 1) * piece],
            w_ref[p * piece : (p + 1) * piece, :],
            preferred_element_type=jnp.float32,
        )
        total = part if total is None else total + part
    o_ref[...] = total


def local_attention(query, new_key, new_value, key_cache, value_cache, lengths, out_weight):
    row_count, local_width = query.shape
    cache_len = key_cache.shape[1]
    vmem = pl.BlockSpec(memory_space=pltpu.VMEM)
    return pl.pallas_call(
        attention_kernel,
        out_shape=jax.ShapeDtypeStruct((row_count, out_weight.shape[1]), jnp.float32),
        in_specs=[pl.BlockSpec(memory_space=pltpu.SMEM)] + [vmem] * 5 + [pl.BlockSpec(memory_space=pl.ANY)],
        out_specs=vmem,
        scratch_shapes=[
            pltpu.VMEM((row_count, local_width), jnp.bfloat16),
            pltpu.VMEM(out_weight.shape, out_weight.dtype),
            pltpu.SemaphoreType.DMA((4,)),
        ],
        cost_estimate=pl.CostEstimate(
            flops=4 * row_count * (local_width // HD) * cache_len * local_width,
            transcendentals=row_count * (local_width // HD) * (cache_len + 1),
            bytes_accessed=2 * key_cache.size * 2 + 4 * query.size * 2 + out_weight.size * 2,
        ),
    )(
        lengths,
        query,
        new_key,
        new_value,
        jnp.swapaxes(key_cache, 1, 2),
        jnp.swapaxes(value_cache, 1, 2),
        out_weight,
    )


def slot_tables(block_ids, block_weights, capacity):
    blocks, rows, picks = block_ids.shape
    expert_hit = block_ids[..., None] == jnp.arange(EXPERTS, dtype=jnp.int32)
    flat_hits = expert_hit.reshape(blocks, rows * picks, EXPERTS).astype(jnp.int32)
    earlier = jnp.cumsum(flat_hits, axis=1) - flat_hits
    slot_index = jnp.sum(earlier * flat_hits, axis=-1).reshape(blocks, rows, picks)
    slot_hit = slot_index[..., None] == jnp.arange(capacity, dtype=jnp.int32)
    pair_hit = expert_hit[..., :, None] & slot_hit[..., None, :]
    selector = jnp.any(pair_hit, axis=2).astype(jnp.bfloat16)
    combiner = jnp.sum(jnp.where(pair_hit, block_weights[..., None, None], 0.0), axis=2)
    return (selector, combiner)


def shards(
    query,
    new_key,
    new_value,
    key_cache,
    value_cache,
    lengths,
    resid,
    out_weight,
    norm_gain,
    expert_ids,
    route_weight,
    gate_weight,
    up_weight,
    down_weight,
):
    row_count = query.shape[0]
    proj_part = local_attention(
        query, new_key, new_value, key_cache, value_cache, lengths, out_weight
    )
    model_width = out_weight.shape[1]
    share = model_width // lax.axis_size("tp")
    col_start = lax.axis_index("tp") * share
    resid_float = resid.astype(jnp.float32)
    tp_count = lax.axis_size("tp")
    proj_all = lax.all_to_all(
        jnp.broadcast_to(proj_part[None], (tp_count,) + proj_part.shape),
        "tp",
        split_axis=0,
        concat_axis=0,
        tiled=True,
    )
    hidden_full = resid_float + jnp.sum(proj_all, axis=0)
    mean_square = jnp.mean(hidden_full * hidden_full, axis=1)
    inv_rms = lax.rsqrt(mean_square + 1e-05)
    hidden_state = lax.dynamic_slice_in_dim(hidden_full, col_start, share, 1)
    normed = (hidden_state * inv_rms[:, None] * norm_gain[None, :]).astype(jnp.bfloat16)
    req_count = lax.axis_size("req")
    group_size = req_count // EXPERTS
    capacity = max(2, row_count // 2)
    first_row = lax.axis_index("req") * row_count
    my_ids = lax.dynamic_slice_in_dim(expert_ids, first_row, row_count, 0)
    my_weights = lax.dynamic_slice_in_dim(route_weight, first_row, row_count, 0)
    selector, combiner = slot_tables(my_ids[None], my_weights[None], capacity)
    expert_rows = jnp.einsum(
        "tec,tf->ecf", selector[0], normed, preferred_element_type=jnp.float32
    ).astype(jnp.bfloat16)
    outgoing = jnp.repeat(expert_rows, group_size, axis=0)
    arrived = lax.all_to_all(outgoing, "req", split_axis=0, concat_axis=0, tiled=True)
    token_rows = arrived.reshape(req_count * capacity, share)
    paired_weight = jnp.concatenate([gate_weight, up_weight], axis=1)
    both = jnp.dot(token_rows, paired_weight, preferred_element_type=jnp.float32).astype(
        jnp.bfloat16
    )
    both = jnp.broadcast_to(both[None], (tp_count,) + both.shape)
    both = lax.all_to_all(both, "tp", split_axis=0, concat_axis=0, tiled=True)
    summed = jnp.sum(both.astype(jnp.float32), axis=0)
    hidden_units = gate_weight.shape[1]
    activ = (jax.nn.silu(summed[:, :hidden_units]) * summed[:, hidden_units:]).astype(jnp.bfloat16)
    partial_out = (
        jnp.dot(activ, down_weight, preferred_element_type=jnp.float32)
        .astype(jnp.bfloat16)
        .reshape(req_count, capacity, share)
    )
    returned = lax.all_to_all(partial_out, "req", split_axis=0, concat_axis=0, tiled=True)
    grouped = jnp.sum(
        returned.reshape(EXPERTS, group_size, capacity, share).astype(jnp.float32), axis=1
    )
    moe_sum = jnp.einsum("tec,ecf->tf", combiner[0], grouped, precision=lax.Precision.HIGHEST)
    return (hidden_state + moe_sum).astype(jnp.bfloat16)


def solution(mesh):
    placed = (
        P("req", "tp"),
        P("req", "tp"),
        P("req", "tp"),
        P("req", None, "tp"),
        P("req", None, "tp"),
        P("req"),
        P("req", None),
        P("tp", None),
        P("tp"),
        P(),
        P(),
        P("tp", "req"),
        P("tp", "req"),
        P("req", "tp"),
    )
    return jax.shard_map(
        shards, mesh=mesh, in_specs=placed, out_specs=P("req", "tp"), check_vma=False
    )
```

```python
import jax
import jax.numpy as jnp
from jax import lax
from jax.sharding import PartitionSpec as P
from jax.experimental import pallas as pl
from jax.experimental.pallas import tpu as pltpu

HD = 64
EXPERTS = 8


def attention_kernel(len_ref, q_ref, nk_ref, nv_ref, k_ref, v_ref, w_hbm, o_ref, attn_ref, w_ref, w_sem):
    pieces = w_sem.shape[0]
    piece = w_ref.shape[0] // pieces
    weight_copies = [
        pltpu.make_async_copy(
            w_hbm.at[pl.ds(p * piece, piece)], w_ref.at[pl.ds(p * piece, piece)], w_sem.at[p]
        )
        for p in range(pieces)
    ]
    for weight_copy in weight_copies:
        weight_copy.start()
    row_count, local_width = q_ref.shape
    head_count = local_width // HD
    cache_len = k_ref.shape[2]
    pair_count = row_count * head_count
    score_scale = HD ** (-0.5)
    pair_row = lax.broadcasted_iota(jnp.int32, (pair_count, row_count), 0) // head_count
    pick_row = (pair_row == lax.broadcasted_iota(jnp.int32, (pair_count, row_count), 1)).astype(
        jnp.bfloat16
    )
    lane_head = lax.broadcasted_iota(jnp.int32, (pair_count, local_width), 1) // HD
    pair_head = lax.broadcasted_iota(jnp.int32, (pair_count, local_width), 0) % head_count
    head_mask = lane_head == pair_head
    query_rows = jnp.dot(pick_row, q_ref[...], preferred_element_type=jnp.float32)
    new_key_rows = jnp.dot(pick_row, nk_ref[...], preferred_element_type=jnp.float32)
    masked_query = jnp.where(head_mask, query_rows, 0.0)
    all_keys = jnp.concatenate([k_ref[r] for r in range(row_count)], axis=1)
    all_values = jnp.concatenate([v_ref[r] for r in range(row_count)], axis=1)
    scores = (
        jnp.dot(masked_query.astype(jnp.bfloat16), all_keys, preferred_element_type=jnp.float32)
        * score_scale
    )
    own_score = jnp.sum(masked_query * new_key_rows, axis=1, keepdims=True) * score_scale
    column = lax.broadcasted_iota(jnp.int32, (pair_count, row_count * cache_len), 1)
    owner = lax.broadcasted_iota(jnp.int32, (pair_count, row_count * cache_len), 0) // head_count
    row_length = jnp.zeros((pair_count, row_count * cache_len), jnp.int32)
    for r in range(row_count):
        row_length = jnp.where(owner == r, len_ref[r], row_length)
    valid = (column // cache_len == owner) & (column % cache_len < row_length)
    scores = jnp.where(valid, scores, -jnp.inf)
    highest = jnp.maximum(jnp.max(scores, axis=1, keepdims=True), own_score)
    cached_exp = jnp.exp(scores - highest)
    own_exp = jnp.exp(own_score - highest)
    denominator = jnp.sum(cached_exp, axis=1, keepdims=True) + own_exp
    cached_prob = (cached_exp / denominator).astype(jnp.bfloat16)
    own_prob = (own_exp / denominator).astype(jnp.bfloat16).astype(jnp.float32)
    mixed_heads = lax.dot_general(
        cached_prob, all_values, (((1,), (1,)), ((), ())), preferred_element_type=jnp.float32
    )
    mixed_heads = jnp.where(head_mask, mixed_heads, 0.0)
    own_lanes = jnp.where(head_mask, own_prob, 0.0)
    new_values = nv_ref[...].astype(jnp.float32)
    for r in range(row_count):
        rows = slice(r * head_count, (r + 1) * head_count)
        mixed = jnp.sum(mixed_heads[rows], axis=0, keepdims=True)
        own = jnp.sum(own_lanes[rows], axis=0, keepdims=True)
        attn_ref[r : r + 1, :] = (mixed + own * new_values[r : r + 1, :]).astype(attn_ref.dtype)
    attn = attn_ref[...]
    total = None
    for p, weight_copy in enumerate(weight_copies):
        weight_copy.wait()
        part = jnp.dot(
            attn[:, p * piece : (p + 1) * piece],
            w_ref[p * piece : (p + 1) * piece, :],
            preferred_element_type=jnp.float32,
        )
        total = part if total is None else total + part
    o_ref[...] = total


def local_attention(query, new_key, new_value, key_cache, value_cache, lengths, out_weight):
    row_count, local_width = query.shape
    cache_len = key_cache.shape[1]
    vmem = pl.BlockSpec(memory_space=pltpu.VMEM)
    return pl.pallas_call(
        attention_kernel,
        out_shape=jax.ShapeDtypeStruct((row_count, out_weight.shape[1]), jnp.float32),
        in_specs=[pl.BlockSpec(memory_space=pltpu.SMEM)] + [vmem] * 5 + [pl.BlockSpec(memory_space=pl.ANY)],
        out_specs=vmem,
        scratch_shapes=[
            pltpu.VMEM((row_count, local_width), jnp.bfloat16),
            pltpu.VMEM(out_weight.shape, out_weight.dtype),
            pltpu.SemaphoreType.DMA((4,)),
        ],
        cost_estimate=pl.CostEstimate(
            flops=4 * row_count * (local_width // HD) * cache_len * local_width,
            transcendentals=row_count * (local_width // HD) * (cache_len + 1),
            bytes_accessed=2 * key_cache.size * 2 + 4 * query.size * 2 + out_weight.size * 2,
        ),
    )(
        lengths,
        query,
        new_key,
        new_value,
        jnp.swapaxes(key_cache, 1, 2),
        jnp.swapaxes(value_cache, 1, 2),
        out_weight,
    )


def slot_tables(block_ids, block_weights, capacity):
    blocks, rows, picks = block_ids.shape
    expert_hit = block_ids[..., None] == jnp.arange(EXPERTS, dtype=jnp.int32)
    flat_hits = expert_hit.reshape(blocks, rows * picks, EXPERTS).astype(jnp.int32)
    earlier = jnp.cumsum(flat_hits, axis=1) - flat_hits
    slot_index = jnp.sum(earlier * flat_hits, axis=-1).reshape(blocks, rows, picks)
    slot_hit = slot_index[..., None] == jnp.arange(capacity, dtype=jnp.int32)
    pair_hit = expert_hit[..., :, None] & slot_hit[..., None, :]
    selector = jnp.any(pair_hit, axis=2).astype(jnp.bfloat16)
    combiner = jnp.sum(jnp.where(pair_hit, block_weights[..., None, None], 0.0), axis=2)
    return (selector, combiner)


def shards(
    query,
    new_key,
    new_value,
    key_cache,
    value_cache,
    lengths,
    resid,
    out_weight,
    norm_gain,
    expert_ids,
    route_weight,
    gate_weight,
    up_weight,
    down_weight,
):
    row_count = query.shape[0]
    proj_part = local_attention(
        query, new_key, new_value, key_cache, value_cache, lengths, out_weight
    )
    model_width = out_weight.shape[1]
    share = model_width // lax.axis_size("tp")
    col_start = lax.axis_index("tp") * share
    resid_float = resid.astype(jnp.float32)
    tp_count = lax.axis_size("tp")
    proj_all = lax.all_to_all(
        jnp.broadcast_to(proj_part[None], (tp_count,) + proj_part.shape),
        "tp",
        split_axis=0,
        concat_axis=0,
        tiled=True,
    )
    hidden_full = resid_float + jnp.sum(proj_all, axis=0)
    mean_square = jnp.mean(hidden_full * hidden_full, axis=1)
    inv_rms = lax.rsqrt(mean_square + 1e-05)
    hidden_state = lax.dynamic_slice_in_dim(hidden_full, col_start, share, 1)
    normed = (hidden_state * inv_rms[:, None] * norm_gain[None, :]).astype(jnp.bfloat16)
    req_count = lax.axis_size("req")
    group_size = req_count // EXPERTS
    capacity = max(2, row_count // 2)
    first_row = lax.axis_index("req") * row_count
    my_ids = lax.dynamic_slice_in_dim(expert_ids, first_row, row_count, 0)
    my_weights = lax.dynamic_slice_in_dim(route_weight, first_row, row_count, 0)
    selector, combiner = slot_tables(my_ids[None], my_weights[None], capacity)
    expert_rows = jnp.einsum(
        "tec,tf->ecf", selector[0], normed, preferred_element_type=jnp.float32
    ).astype(jnp.bfloat16)
    outgoing = jnp.repeat(expert_rows, group_size, axis=0)
    arrived = lax.all_to_all(outgoing, "req", split_axis=0, concat_axis=0, tiled=True)
    token_rows = arrived.reshape(req_count * capacity, share)
    chunk = gate_weight.shape[1] // tp_count
    paired_weight = jnp.concatenate(
        [
            gate_weight.reshape(share, tp_count, chunk),
            up_weight.reshape(share, tp_count, chunk),
        ],
        axis=2,
    )
    both = jnp.einsum(
        "sf,ftk->tsk", token_rows, paired_weight, preferred_element_type=jnp.float32
    ).astype(jnp.bfloat16)
    both = lax.all_to_all(both, "tp", split_axis=0, concat_axis=0, tiled=True)
    summed = jnp.sum(both.astype(jnp.float32), axis=0)
    activ_chunk = (jax.nn.silu(summed[:, :chunk]) * summed[:, chunk:]).astype(jnp.bfloat16)
    activ_all = lax.all_to_all(
        jnp.broadcast_to(activ_chunk[None], (tp_count,) + activ_chunk.shape),
        "tp",
        split_axis=0,
        concat_axis=0,
        tiled=True,
    )
    activ = jnp.moveaxis(activ_all, 0, 1).reshape(activ_chunk.shape[0], tp_count * chunk)
    partial_out = (
        jnp.dot(activ, down_weight, preferred_element_type=jnp.float32)
        .astype(jnp.bfloat16)
        .reshape(req_count, capacity, share)
    )
    returned = lax.all_to_all(partial_out, "req", split_axis=0, concat_axis=0, tiled=True)
    grouped = jnp.sum(
        returned.reshape(EXPERTS, group_size, capacity, share).astype(jnp.float32), axis=1
    )
    moe_sum = jnp.einsum("tec,ecf->tf", combiner[0], grouped, precision=lax.Precision.HIGHEST)
    return (hidden_state + moe_sum).astype(jnp.bfloat16)


def solution(mesh):
    placed = (
        P("req", "tp"),
        P("req", "tp"),
        P("req", "tp"),
        P("req", None, "tp"),
        P("req", None, "tp"),
        P("req"),
        P("req", None),
        P("tp", None),
        P("tp"),
        P(),
        P(),
        P("tp", "req"),
        P("tp", "req"),
        P("req", "tp"),
    )
    return jax.shard_map(
        shards, mesh=mesh, in_specs=placed, out_specs=P("req", "tp"), check_vma=False
    )
```

```python
import jax
import jax.numpy as jnp
from jax import lax
from jax.sharding import PartitionSpec as P
from jax.experimental import pallas as pl
from jax.experimental.pallas import tpu as pltpu

HD = 64
EXPERTS = 8


def attention_kernel(len_ref, q_ref, nk_ref, nv_ref, k_ref, v_ref, w_hbm, o_ref, attn_ref, w_ref, w_sem):
    pieces = w_sem.shape[0]
    piece = w_ref.shape[0] // pieces
    weight_copies = [
        pltpu.make_async_copy(
            w_hbm.at[pl.ds(p * piece, piece)], w_ref.at[pl.ds(p * piece, piece)], w_sem.at[p]
        )
        for p in range(pieces)
    ]
    for weight_copy in weight_copies:
        weight_copy.start()
    row_count, local_width = q_ref.shape
    head_count = local_width // HD
    cache_len = k_ref.shape[2]
    pair_count = row_count * head_count
    score_scale = HD ** (-0.5)
    pair_row = lax.broadcasted_iota(jnp.int32, (pair_count, row_count), 0) // head_count
    pick_row = (pair_row == lax.broadcasted_iota(jnp.int32, (pair_count, row_count), 1)).astype(
        jnp.bfloat16
    )
    lane_head = lax.broadcasted_iota(jnp.int32, (pair_count, local_width), 1) // HD
    pair_head = lax.broadcasted_iota(jnp.int32, (pair_count, local_width), 0) % head_count
    head_mask = lane_head == pair_head
    query_rows = jnp.dot(pick_row, q_ref[...], preferred_element_type=jnp.float32)
    new_key_rows = jnp.dot(pick_row, nk_ref[...], preferred_element_type=jnp.float32)
    masked_query = jnp.where(head_mask, query_rows, 0.0)
    all_keys = jnp.concatenate([k_ref[r] for r in range(row_count)], axis=1)
    all_values = jnp.concatenate([v_ref[r] for r in range(row_count)], axis=1)
    scores = (
        jnp.dot(masked_query.astype(jnp.bfloat16), all_keys, preferred_element_type=jnp.float32)
        * score_scale
    )
    own_score = jnp.sum(masked_query * new_key_rows, axis=1, keepdims=True) * score_scale
    column = lax.broadcasted_iota(jnp.int32, (pair_count, row_count * cache_len), 1)
    owner = lax.broadcasted_iota(jnp.int32, (pair_count, row_count * cache_len), 0) // head_count
    row_length = jnp.zeros((pair_count, row_count * cache_len), jnp.int32)
    for r in range(row_count):
        row_length = jnp.where(owner == r, len_ref[r], row_length)
    valid = (column // cache_len == owner) & (column % cache_len < row_length)
    scores = jnp.where(valid, scores, -jnp.inf)
    highest = jnp.maximum(jnp.max(scores, axis=1, keepdims=True), own_score)
    cached_exp = jnp.exp(scores - highest)
    own_exp = jnp.exp(own_score - highest)
    denominator = jnp.sum(cached_exp, axis=1, keepdims=True) + own_exp
    cached_prob = (cached_exp / denominator).astype(jnp.bfloat16)
    own_prob = (own_exp / denominator).astype(jnp.bfloat16).astype(jnp.float32)
    mixed_heads = lax.dot_general(
        cached_prob, all_values, (((1,), (1,)), ((), ())), preferred_element_type=jnp.float32
    )
    mixed_heads = jnp.where(head_mask, mixed_heads, 0.0)
    own_lanes = jnp.where(head_mask, own_prob, 0.0)
    new_values = nv_ref[...].astype(jnp.float32)
    for r in range(row_count):
        rows = slice(r * head_count, (r + 1) * head_count)
        mixed = jnp.sum(mixed_heads[rows], axis=0, keepdims=True)
        own = jnp.sum(own_lanes[rows], axis=0, keepdims=True)
        attn_ref[r : r + 1, :] = (mixed + own * new_values[r : r + 1, :]).astype(attn_ref.dtype)
    attn = attn_ref[...]
    total = None
    for p, weight_copy in enumerate(weight_copies):
        weight_copy.wait()
        part = jnp.dot(
            attn[:, p * piece : (p + 1) * piece],
            w_ref[p * piece : (p + 1) * piece, :],
            preferred_element_type=jnp.float32,
        )
        total = part if total is None else total + part
    for copy_index in range(o_ref.shape[0]):
        o_ref[copy_index] = total


def local_attention(query, new_key, new_value, key_cache, value_cache, lengths, out_weight, copies):
    row_count, local_width = query.shape
    cache_len = key_cache.shape[1]
    vmem = pl.BlockSpec(memory_space=pltpu.VMEM)
    return pl.pallas_call(
        attention_kernel,
        out_shape=jax.ShapeDtypeStruct((copies, row_count, out_weight.shape[1]), jnp.float32),
        in_specs=[pl.BlockSpec(memory_space=pltpu.SMEM)] + [vmem] * 5 + [pl.BlockSpec(memory_space=pl.ANY)],
        out_specs=vmem,
        scratch_shapes=[
            pltpu.VMEM((row_count, local_width), jnp.bfloat16),
            pltpu.VMEM(out_weight.shape, out_weight.dtype),
            pltpu.SemaphoreType.DMA((4,)),
        ],
        cost_estimate=pl.CostEstimate(
            flops=4 * row_count * (local_width // HD) * cache_len * local_width,
            transcendentals=row_count * (local_width // HD) * (cache_len + 1),
            bytes_accessed=2 * key_cache.size * 2 + 4 * query.size * 2 + out_weight.size * 2,
        ),
    )(
        lengths,
        query,
        new_key,
        new_value,
        jnp.swapaxes(key_cache, 1, 2),
        jnp.swapaxes(value_cache, 1, 2),
        out_weight,
    )


def slot_tables(block_ids, block_weights, capacity):
    blocks, rows, picks = block_ids.shape
    expert_hit = block_ids[..., None] == jnp.arange(EXPERTS, dtype=jnp.int32)
    flat_hits = expert_hit.reshape(blocks, rows * picks, EXPERTS).astype(jnp.int32)
    earlier = jnp.cumsum(flat_hits, axis=1) - flat_hits
    slot_index = jnp.sum(earlier * flat_hits, axis=-1).reshape(blocks, rows, picks)
    slot_hit = slot_index[..., None] == jnp.arange(capacity, dtype=jnp.int32)
    pair_hit = expert_hit[..., :, None] & slot_hit[..., None, :]
    selector = jnp.any(pair_hit, axis=2).astype(jnp.bfloat16)
    combiner = jnp.sum(jnp.where(pair_hit, block_weights[..., None, None], 0.0), axis=2)
    return (selector, combiner)


def shards(
    query,
    new_key,
    new_value,
    key_cache,
    value_cache,
    lengths,
    resid,
    out_weight,
    norm_gain,
    expert_ids,
    route_weight,
    gate_weight,
    up_weight,
    down_weight,
):
    row_count = query.shape[0]
    tp_count = lax.axis_size("tp")
    proj_copies = local_attention(
        query, new_key, new_value, key_cache, value_cache, lengths, out_weight, tp_count
    )
    model_width = out_weight.shape[1]
    share = model_width // lax.axis_size("tp")
    col_start = lax.axis_index("tp") * share
    resid_float = resid.astype(jnp.float32)
    proj_all = lax.all_to_all(
        proj_copies,
        "tp",
        split_axis=0,
        concat_axis=0,
        tiled=True,
    )
    hidden_full = resid_float + jnp.sum(proj_all, axis=0)
    mean_square = jnp.mean(hidden_full * hidden_full, axis=1)
    inv_rms = lax.rsqrt(mean_square + 1e-05)
    hidden_state = lax.dynamic_slice_in_dim(hidden_full, col_start, share, 1)
    normed = (hidden_state * inv_rms[:, None] * norm_gain[None, :]).astype(jnp.bfloat16)
    req_count = lax.axis_size("req")
    group_size = req_count // EXPERTS
    capacity = max(2, row_count // 2)
    first_row = lax.axis_index("req") * row_count
    my_ids = lax.dynamic_slice_in_dim(expert_ids, first_row, row_count, 0)
    my_weights = lax.dynamic_slice_in_dim(route_weight, first_row, row_count, 0)
    selector, combiner = slot_tables(my_ids[None], my_weights[None], capacity)
    expert_rows = jnp.einsum(
        "tec,tf->ecf", selector[0], normed, preferred_element_type=jnp.float32
    ).astype(jnp.bfloat16)
    outgoing = jnp.repeat(expert_rows, group_size, axis=0)
    arrived = lax.all_to_all(outgoing, "req", split_axis=0, concat_axis=0, tiled=True)
    token_rows = arrived.reshape(req_count * capacity, share)
    chunk = gate_weight.shape[1] // tp_count
    paired_weight = jnp.concatenate(
        [
            gate_weight.reshape(share, tp_count, chunk),
            up_weight.reshape(share, tp_count, chunk),
        ],
        axis=2,
    )
    both = jnp.einsum(
        "sf,ftk->tsk", token_rows, paired_weight, preferred_element_type=jnp.float32
    ).astype(jnp.bfloat16)
    both = lax.all_to_all(both, "tp", split_axis=0, concat_axis=0, tiled=True)
    summed = jnp.sum(both.astype(jnp.float32), axis=0)
    activ_chunk = (jax.nn.silu(summed[:, :chunk]) * summed[:, chunk:]).astype(jnp.bfloat16)
    activ_all = lax.all_to_all(
        jnp.broadcast_to(activ_chunk[None], (tp_count,) + activ_chunk.shape),
        "tp",
        split_axis=0,
        concat_axis=0,
        tiled=True,
    )
    activ = jnp.moveaxis(activ_all, 0, 1).reshape(activ_chunk.shape[0], tp_count * chunk)
    partial_out = (
        jnp.dot(activ, down_weight, preferred_element_type=jnp.float32)
        .astype(jnp.bfloat16)
        .reshape(req_count, capacity, share)
    )
    returned = lax.all_to_all(partial_out, "req", split_axis=0, concat_axis=0, tiled=True)
    grouped = jnp.sum(
        returned.reshape(EXPERTS, group_size, capacity, share).astype(jnp.float32), axis=1
    )
    moe_sum = jnp.einsum("tec,ecf->tf", combiner[0], grouped, precision=lax.Precision.HIGHEST)
    return (hidden_state + moe_sum).astype(jnp.bfloat16)


def solution(mesh):
    placed = (
        P("req", "tp"),
        P("req", "tp"),
        P("req", "tp"),
        P("req", None, "tp"),
        P("req", None, "tp"),
        P("req"),
        P("req", None),
        P("tp", None),
        P("tp"),
        P(),
        P(),
        P("tp", "req"),
        P("tp", "req"),
        P("req", "tp"),
    )
    return jax.shard_map(
        shards, mesh=mesh, in_specs=placed, out_specs=P("req", "tp"), check_vma=False
    )
```
